128 devices in a mesh: dom: 16 (over x, z_hi, core), cls: 8 (over z_lo, y).
Axes of the slice: x: 4, y: 4, z: 4 (z_hi: 2, z_lo: 2; z = z_hi * 2 + z_lo), core: 2. Of those that a mesh axis runs over, the one named last changes fastest.
Arguments:
- particles: bfloat16 [2048, 16384], P(('dom', 'cls')), may hold values from -6 to 6
- averages: float32 [256, 16384], P('cls'), may hold values from -4 to 4
- prior_mass: float32 [256], P('cls'), may hold values from 1 to 8
- group_ids: int32 [4, 2048, 1], P(None, ('dom', 'cls')), may hold values from 0 to 7; in each aligned block of 16 rows (0 to 15, 16 to 31, ..., all dimensions but the last counted through in order) at most 6 rows name the same one
- class_ids: int32 [4, 2048], P(None, ('dom', 'cls')), may hold values from 0 to 31
- rot_ids: int32 [4, 2048], P(None, ('dom', 'cls')), may hold values from 0 to 63
- weights: bfloat16 [4, 2048], P(None, ('dom', 'cls')), may hold values from 0.25 to 4
- owners: int32 [4], replicated, may hold values from 0 to 7
Outputs:
- scores: float32 [4, 2048, 2048], P(None, ('dom', 'cls'))
- final_averages: float32 [256, 16384], P('cls')
The draws below stay inside these ranges and needn't reach their ends.
Inputs may be any that keep to these rules, and one draw needn't show every extreme that they name: `group_ids`: in every step, at most 6 of the 16 particles of one device name one class group; in every step some device's particles reach 6 for some group.
All inputs are finite; a program needn't handle non-finite values.
Results may differ from the reference program's by a relative error of at most 0.0027.
Values may be sent and summed in bfloat16 or wider, within the bound.
No kernel may reach another device: no remote copies, remote signals or barrier semaphores. Data moves between devices by JAX's collectives and lax.ppermute only.
A program may use at most 256 MiB of HBM per device.

```python
import math
import jax
import jax.numpy as jnp
import numpy as np
from jax import lax

RADII = 128
ANGLES = 128
ROT = 64
CLS_DEV = 32
PD = 16
STEPS = 4
CAP = 6
ASTEP = 2
CLASSES = 256
PARTICLES = 2048
N_CLS = 8


def with_ends(drawn, rng, low, largest):
    longest = drawn.shape.index(max(drawn.shape))
    spots = []
    for shift in (0, 1):
        where = [jax.random.randint(jax.random.fold_in(rng, axis), (), 0, length) for axis, length in enumerate(drawn.shape)]
        where[longest] = (where[longest] + shift) % drawn.shape[longest]
        spots.append(tuple(where))
    return drawn.at[spots[0]].set(low).at[spots[1]].set(largest)


def level_of(stream_key, shape, shards, low, high):
    loudness, own = 1.0, jax.random.fold_in(stream_key, 6)
    for dim, blocks in shards:
        steps = jnp.exp(jax.random.uniform(jax.random.fold_in(own, dim), (blocks,), jnp.float32, low / len(shards), high / len(shards)))
        loudness = loudness * jnp.repeat(steps, shape[dim] // blocks).reshape([-1 if axis == dim else 1 for axis in range(len(shape))])
    return loudness


def cumulative_ranks(count, slope):
    portions = [(1 << 20) // math.isqrt(standing ** slope) + 1 for standing in range(1, count + 1)]
    spread = 1 + sum(portions) // (1 << 30)
    return np.cumsum(np.array([max(1, weight // spread) for weight in portions]))


def ranked_ids(own_key, dims, number_of, slope):
    listing = cumulative_ranks(number_of, slope)
    lot = jax.random.randint(jax.random.fold_in(own_key, 1), dims, 0, int(listing[number_of - 1]))
    grade = jnp.searchsorted(jnp.asarray(listing, jnp.int32), lot, side="right")
    return jax.random.permutation(jax.random.fold_in(own_key, 2), number_of)[grade].astype(jnp.int32)


def routed_block(key, own, number, rows, amount, top, bound, skew):
    ranking = jax.random.permutation(key, amount)
    crowded, common = portions_of(amount, rows * top, bound, skew, True), portions_of(amount, rows * top, bound, skew, False)
    places = jnp.arange(amount)

    def named(lengths, turn):
        used = int((lengths > 0).sum())
        fixed = max(1, used // 4)
        passed = fixed + (places - fixed + turn * (used - fixed)) % max(1, amount - fixed)
        return jnp.zeros((amount,), jnp.int32).at[ranking[jnp.where(places < fixed, places, passed)]].set(jnp.asarray(lengths, jnp.int32))

    lengths = jnp.where(number % 4 == 0, named(crowded, number // 4), named(common, number - number // 4 - 1))
    mixed = jax.random.permutation(jax.random.fold_in(own, 3), amount)
    donor, sink = mixed[0:amount // 2 * 2:2], mixed[1:amount // 2 * 2:2]
    slack = jnp.minimum(lengths[donor] - 1, bound - lengths[sink]) // 2
    slack = jnp.where((donor == ranking[0]) | (sink == ranking[0]) | (lengths[sink] == 0), 0, jnp.maximum(slack, 0))
    passed = jax.random.randint(jax.random.fold_in(own, 4), (amount // 2,), 0, 1 << 20) % (slack + 1)
    lengths = lengths.at[donor].add(-passed).at[sink].add(passed)
    items = jnp.searchsorted(jnp.cumsum(lengths), jnp.arange(rows * top), side="right").astype(jnp.int32)
    listing = items.reshape(top, rows).T
    listing = listing[jax.random.permutation(jax.random.fold_in(own, 1), rows)]
    turn = jax.random.randint(jax.random.fold_in(own, 2), (rows, 1), 0, top)
    return jnp.take_along_axis(listing, (jnp.arange(top)[None, :] + turn) % top, axis=1)


def portions_of(amount, total, bound, lean, full):
    weights = [(1 << 20) // math.isqrt(grade ** lean) + 1 for grade in range(1, amount + 1)]
    largest = bound if full else min(bound, max(-(-total // amount), total * weights[0] // sum(weights)))
    least = 1 if total - largest >= amount - 1 else 0
    holding, surplus = [largest] + [least] * (amount - 1), total - largest - least * (amount - 1)
    while surplus > 0:
        free = [i for i in range(1, amount) if holding[i] < largest] or [i for i in range(1, amount) if holding[i] < bound]
        pool, left = sum([weights[i] for i in free]), surplus
        for i in free:
            addition = min(bound - holding[i], max(1, left * weights[i] // pool), surplus)
            holding[i] = holding[i] + addition
            surplus = surplus - addition
    return np.array(holding)


def centred(own_key, dims, width, bound, shards=(), held_as=jnp.bfloat16):
    values = width * jax.random.normal(own_key, dims, jnp.float32)
    if shards:
        values = values * level_of(own_key, dims, shards, -0.22, 0.18)
    return jnp.clip(values, -bound, bound).astype(held_as)


def setup_inputs(seed: int = 0) -> dict:
    keys = jax.random.split(jax.random.key(seed), 9)
    particles = centred(keys[0], (PARTICLES, RADII * ANGLES), 1.0, 6.0, ((0, 128),))
    averages = centred(keys[1], (CLASSES, RADII * ANGLES), 0.5, 4.0, ((0, 8),), jnp.float32)
    prior_mass = jnp.clip(jnp.exp(math.log(8.0) - 2.0794415 * jax.random.uniform(keys[2], (CLASSES,), jnp.float32) ** level_of(keys[2], (CLASSES,), ((0, 8),), -0.2, 0.2)), 1.0, 8.0)
    group_ids_keys = jax.random.split(jax.random.fold_in(keys[3], 1), STEPS * PARTICLES // PD)
    group_ids_turns = jax.random.permutation(jax.random.fold_in(keys[3], 3), STEPS * PARTICLES // PD)
    group_ids = jax.vmap(lambda own, number: routed_block(jax.random.fold_in(keys[3], 2), own, number, PD, N_CLS, 1, CAP, 2))(group_ids_keys, group_ids_turns).reshape((STEPS, PARTICLES, 1))
    class_ids = with_ends(ranked_ids(keys[4], (STEPS, PARTICLES), CLS_DEV, 2), jax.random.fold_in(keys[4], 3), 0, CLS_DEV - 1).astype(jnp.int32)
    rot_ids = with_ends(jax.random.randint(keys[5], (STEPS, PARTICLES), 0, ROT), jax.random.fold_in(keys[5], 1), 0, ROT - 1).astype(jnp.int32)
    weights = jnp.clip(jnp.exp(math.log(4.0) - 2.7725887 * jax.random.uniform(keys[6], (STEPS, PARTICLES), jnp.float32) ** level_of(keys[6], (STEPS, PARTICLES), ((1, 128),), -0.2, 0.2)), 0.25, 4.0).astype(jnp.bfloat16)
    owners = with_ends(jax.random.randint(keys[7], (STEPS,), 0, N_CLS), jax.random.fold_in(keys[7], 1), 0, N_CLS - 1).astype(jnp.int32)
    return dict(particles=particles, averages=averages, prior_mass=prior_mass, group_ids=group_ids, class_ids=class_ids, rot_ids=rot_ids, weights=weights, owners=owners)


def rotate_each(images, shifts):
    angle_idx = jnp.arange(ANGLES, dtype=jnp.int32)
    index = (angle_idx[None, :] - shifts[:, None]) % ANGLES
    return jnp.take_along_axis(images, index[:, None, :], axis=2)

def reference(particles, averages, prior_mass, group_ids, class_ids, rot_ids, weights, owners):
    pixels = RADII * ANGLES
    cube = particles.reshape(-1, RADII, ANGLES)
    flat = particles
    scale = 1.0 / math.sqrt(pixels)
    current = averages
    all_scores = []
    for step in range(STEPS):
        shifts = (rot_ids[step] * ASTEP).astype(jnp.int32)
        rotated = rotate_each(cube, shifts).reshape(-1, pixels)
        labels = (group_ids[step, :, 0] * CLS_DEV + class_ids[step]).astype(jnp.int32)
        wts = weights[step].astype(jnp.float32)
        terms = rotated.astype(jnp.float32) * wts[:, None]
        totals = jax.ops.segment_sum(terms, labels, num_segments=CLASSES)
        mass = jax.ops.segment_sum(wts, labels, num_segments=CLASSES)
        current = (prior_mass[:, None] * current + totals) / (prior_mass + mass)[:, None]
        start = (owners[step] * CLS_DEV).astype(jnp.int32)
        refs = lax.dynamic_slice_in_dim(current, start, CLS_DEV, 0).astype(jnp.bfloat16)
        ref_cube = refs.reshape(CLS_DEV, RADII, ANGLES)
        blocks = []
        for turn in range(ROT):
            turned = jnp.roll(ref_cube, -turn * ASTEP, axis=2).reshape(CLS_DEV, pixels)
            blocks.append(jnp.dot(flat, turned.T, preferred_element_type=jnp.float32))
        stacked = jnp.stack(blocks, axis=1).reshape(cube.shape[0], ROT * CLS_DEV)
        all_scores.append(stacked * scale)
    return (jnp.stack(all_scores, axis=0), current)
```

```python
import math

import jax
import jax.numpy as jnp
from jax import lax
from jax.sharding import PartitionSpec as P

RADII = 128
ANGLES = 128
ROT = 64
STEPS = 4
ASTEP = 2


def rotate_each(cube, shifts):
    src = jnp.arange(ANGLES, dtype=jnp.int32)
    dst = (src[None, :, None] + shifts[:, None, None]) % ANGLES
    perm = (dst == src[None, None, :]).astype(cube.dtype)
    out = jnp.einsum("iab,ibc->iac", cube, perm, preferred_element_type=jnp.float32)
    return out.astype(cube.dtype)


def per_device(particles, averages, prior_mass, group_ids, class_ids, rot_ids, weights, owners):
    per_dev = particles.shape[0]
    pixels = particles.shape[1]
    groups = lax.axis_size("cls")
    doms = lax.axis_size("dom")
    chunk = pixels // doms
    per_group = averages.shape[0]
    capacity = per_dev * 3 // 8
    slots = groups * capacity
    me_dom = lax.axis_index("dom")
    me_cls = lax.axis_index("cls")
    cube = particles.reshape(per_dev, RADII, ANGLES)
    doubled = jnp.concatenate([cube, cube], axis=2)
    scale = 1.0 / math.sqrt(pixels)
    turns_block = min(ROT, max(8, 512 // per_dev))
    block_starts = list(range(0, ROT, turns_block))

    send_img = []
    send_wts = []
    for step in range(STEPS):
        shifts = rot_ids[step] * ASTEP
        rotated = rotate_each(cube, shifts).reshape(per_dev, pixels)
        target = group_ids[step, :, 0]
        onehot_group = (target[:, None] == jnp.arange(groups, dtype=jnp.int32)[None, :]).astype(
            jnp.int32
        )
        rank = jnp.sum((jnp.cumsum(onehot_group, axis=0) - 1) * onehot_group, axis=1)
        slot_of = target * capacity + rank
        placing = (slot_of[None, :] == jnp.arange(slots, dtype=jnp.int32)[:, None]).astype(
            jnp.bfloat16
        )
        images = jnp.dot(placing, rotated, preferred_element_type=jnp.float32).astype(jnp.bfloat16)
        images = images.reshape(groups, capacity, doms, chunk).transpose(2, 0, 1, 3)
        send_img.append(images)
        class_hot = (
            class_ids[step][:, None] == jnp.arange(per_group, dtype=jnp.int32)[None, :]
        ).astype(jnp.bfloat16)
        weighted_hot = class_hot * weights[step][:, None]
        wts = jnp.dot(placing, weighted_hot, preferred_element_type=jnp.float32).astype(
            jnp.bfloat16
        )
        wts = jnp.broadcast_to(wts.reshape(1, groups, capacity, per_group), (doms, groups, capacity, per_group))
        send_wts.append(wts)
    send_img = jnp.stack(send_img, axis=2).reshape(doms * groups, STEPS, capacity, chunk)
    send_wts = jnp.stack(send_wts, axis=2).reshape(doms * groups, STEPS, capacity, per_group)
    got_img = lax.all_to_all(send_img, ("dom", "cls"), 0, 0, tiled=True)
    got_wts = lax.all_to_all(send_wts, ("dom", "cls"), 0, 0, tiled=True)
    totals = lax.dot_general(
        got_wts, got_img, (((0, 2), (0, 2)), ((1,), (1,))), preferred_element_type=jnp.float32
    )
    mass = jnp.sum(got_wts.astype(jnp.float32), axis=(0, 2))

    current = lax.dynamic_slice_in_dim(averages, me_dom * chunk, chunk, axis=1)
    ref_chunks = []
    for step in range(STEPS):
        current = (prior_mass[:, None] * current + totals[step]) / (prior_mass + mass[step])[:, None]
        piece = current.astype(jnp.bfloat16)
        piece = jnp.where(me_cls == owners[step], piece, jnp.zeros_like(piece))
        ref_chunks.append(piece)
    ref_chunks = lax.psum(jnp.stack(ref_chunks, axis=0), "cls")
    all_refs = lax.all_gather(ref_chunks, "dom", axis=0, tiled=False)
    all_refs = all_refs.transpose(1, 2, 0, 3).reshape(STEPS, per_group, pixels)
    final = lax.all_gather(current, "dom", axis=0, tiled=False)
    final = final.transpose(1, 0, 2).reshape(per_group, pixels)

    all_scores = []
    for step in range(STEPS):
        refs = all_refs[step]
        pieces = []
        for first in block_starts:
            count = min(turns_block, ROT - first)
            views = [
                doubled[:, :, ANGLES - turn * ASTEP : 2 * ANGLES - turn * ASTEP]
                for turn in range(first, first + count)
            ]
            rolled = jnp.stack(views, axis=1).reshape(per_dev * count, pixels)
            product = lax.dot_general(
                rolled, refs, (((1,), (1,)), ((), ())), preferred_element_type=jnp.float32
            )
            pieces.append(product.reshape(per_dev, count * per_group))
        stacked = jnp.concatenate(pieces, axis=1)
        all_scores.append(stacked * scale)
    return (jnp.stack(all_scores, axis=0), final)


def solution(mesh):
    return jax.shard_map(
        per_device,
        mesh=mesh,
        in_specs=(
            P(("dom", "cls"), None),
            P("cls", None),
            P("cls"),
            P(None, ("dom", "cls"), None),
            P(None, ("dom", "cls")),
            P(None, ("dom", "cls")),
            P(None, ("dom", "cls")),
            P(),
        ),
        out_specs=(P(None, ("dom", "cls"), None), P("cls", None)),
        check_vma=False,
    )
```

```python
import math

import jax
import jax.numpy as jnp
from jax import lax
from jax.experimental import pallas as pl
from jax.experimental.pallas import tpu as pltpu
from jax.sharding import PartitionSpec as P

RADII = 128
ANGLES = 128
ROT = 64
STEPS = 4
ASTEP = 2


def _scores_kernel(pt_ref, r_ref, o_ref):
    classes = r_ref.shape[1]
    per_dev = o_ref.shape[2]
    angles = o_ref.shape[3]
    pt = pt_ref[...]

    def body(k, carry):
        g = jnp.dot(pt, r_ref[0, k], preferred_element_type=jnp.float32)
        g = pltpu.roll(g, 0, 1, stride=1, stride_axis=0)
        o_ref[0, k] = jnp.sum(g.reshape(per_dev, angles, angles), axis=1)
        return carry

    lax.fori_loop(0, classes, body, 0)

def shift_scores(cube, refs):
    n, radii, angles = cube.shape
    steps, classes = refs.shape[:2]
    rev = jnp.roll(jnp.flip(cube, axis=2), 1, axis=2)
    pt = rev.transpose(0, 2, 1).reshape(n * angles, radii)
    flops = 2 * steps * classes * n * angles * radii * angles
    return pl.pallas_call(
        _scores_kernel,
        grid=(steps,),
        in_specs=[
            pl.BlockSpec((n * angles, radii), lambda s: (0, 0)),
            pl.BlockSpec((1, classes, radii, angles), lambda s: (s, 0, 0, 0)),
        ],
        out_specs=pl.BlockSpec((1, classes, n, angles), lambda s: (s, 0, 0, 0)),
        out_shape=jax.ShapeDtypeStruct((steps, classes, n, angles), jnp.float32),
        cost_estimate=pl.CostEstimate(flops=flops, transcendentals=0, bytes_accessed=pt.size * 2 + refs.size * 2 + steps * classes * n * angles * 4),
    )(pt, refs)


def rotate_each(cube, shifts):
    src = jnp.arange(ANGLES, dtype=jnp.int32)
    dst = (src[None, :, None] + shifts[:, None, None]) % ANGLES
    perm = (dst == src[None, None, :]).astype(cube.dtype)
    out = jnp.einsum("iab,ibc->iac", cube, perm, preferred_element_type=jnp.float32)
    return out.astype(cube.dtype)


def per_device(particles, averages, prior_mass, group_ids, class_ids, rot_ids, weights, owners):
    per_dev = particles.shape[0]
    pixels = particles.shape[1]
    groups = lax.axis_size("cls")
    doms = lax.axis_size("dom")
    chunk = pixels // doms
    per_group = averages.shape[0]
    capacity = per_dev * 3 // 8
    slots = groups * capacity
    me_dom = lax.axis_index("dom")
    me_cls = lax.axis_index("cls")
    cube = particles.reshape(per_dev, RADII, ANGLES)
    scale = 1.0 / math.sqrt(pixels)

    send_img = []
    send_wts = []
    for step in range(STEPS):
        shifts = rot_ids[step] * ASTEP
        rotated = rotate_each(cube, shifts).reshape(per_dev, pixels)
        target = group_ids[step, :, 0]
        onehot_group = (target[:, None] == jnp.arange(groups, dtype=jnp.int32)[None, :]).astype(
            jnp.int32
        )
        rank = jnp.sum((jnp.cumsum(onehot_group, axis=0) - 1) * onehot_group, axis=1)
        slot_of = target * capacity + rank
        placing = (slot_of[None, :] == jnp.arange(slots, dtype=jnp.int32)[:, None]).astype(
            jnp.bfloat16
        )
        images = jnp.dot(placing, rotated, preferred_element_type=jnp.float32).astype(jnp.bfloat16)
        images = images.reshape(groups, capacity, doms, chunk).transpose(2, 0, 1, 3)
        send_img.append(images)
        class_hot = (
            class_ids[step][:, None] == jnp.arange(per_group, dtype=jnp.int32)[None, :]
        ).astype(jnp.bfloat16)
        weighted_hot = class_hot * weights[step][:, None]
        wts = jnp.dot(placing, weighted_hot, preferred_element_type=jnp.float32).astype(
            jnp.bfloat16
        )
        wts = jnp.broadcast_to(wts.reshape(1, groups, capacity, per_group), (doms, groups, capacity, per_group))
        send_wts.append(wts)
    send_img = jnp.stack(send_img, axis=2).reshape(doms * groups, STEPS, capacity, chunk)
    send_wts = jnp.stack(send_wts, axis=2).reshape(doms * groups, STEPS, capacity, per_group)
    got_img = lax.all_to_all(send_img, ("dom", "cls"), 0, 0, tiled=True)
    got_wts = lax.all_to_all(send_wts, ("dom", "cls"), 0, 0, tiled=True)
    totals = lax.dot_general(
        got_wts, got_img, (((0, 2), (0, 2)), ((1,), (1,))), preferred_element_type=jnp.float32
    )
    mass = jnp.sum(got_wts.astype(jnp.float32), axis=(0, 2))

    current = lax.dynamic_slice_in_dim(averages, me_dom * chunk, chunk, axis=1)
    ref_chunks = []
    for step in range(STEPS):
        current = (prior_mass[:, None] * current + totals[step]) / (prior_mass + mass[step])[:, None]
        piece = current.astype(jnp.bfloat16)
        piece = jnp.where(me_cls == owners[step], piece, jnp.zeros_like(piece))
        ref_chunks.append(piece)
    ref_chunks = lax.psum(jnp.stack(ref_chunks, axis=0), "cls")
    all_refs = lax.all_gather(ref_chunks, "dom", axis=0, tiled=False)
    all_refs = all_refs.transpose(1, 2, 0, 3).reshape(STEPS, per_group, pixels)
    final = lax.all_gather(current, "dom", axis=0, tiled=False)
    final = final.transpose(1, 0, 2).reshape(per_group, pixels)

    shifted = shift_scores(cube, all_refs.reshape(STEPS, per_group, RADII, ANGLES))
    scores = shifted[..., ::ASTEP].transpose(0, 2, 3, 1).reshape(STEPS, per_dev, ROT * per_group)
    return (scores * scale, final)


def solution(mesh):
    return jax.shard_map(
        per_device,
        mesh=mesh,
        in_specs=(
            P(("dom", "cls"), None),
            P("cls", None),
            P("cls"),
            P(None, ("dom", "cls"), None),
            P(None, ("dom", "cls")),
            P(None, ("dom", "cls")),
            P(None, ("dom", "cls")),
            P(),
        ),
        out_specs=(P(None, ("dom", "cls"), None), P("cls", None)),
        check_vma=False,
    )
```

```python
import math

import jax
import jax.numpy as jnp
from jax import lax
from jax.experimental import pallas as pl
from jax.experimental.pallas import tpu as pltpu
from jax.sharding import PartitionSpec as P

RADII = 128
ANGLES = 128
ROT = 64
STEPS = 4
ASTEP = 2


def _scores_kernel(pt_ref, sel_ref, r_ref, o_ref):
    classes = r_ref.shape[1]
    per_dev = o_ref.shape[2]
    lanes = o_ref.shape[3]
    pt = pt_ref[...]
    sel = sel_ref[...]
    rows = pt.shape[0] // per_dev
    parts = sel.shape[1] // lanes

    def body(k, carry):
        split = jnp.dot(r_ref[0, k], sel, preferred_element_type=jnp.float32).astype(pt.dtype)
        rhs = jnp.concatenate([split[:, e * lanes:(e + 1) * lanes] for e in range(parts)], axis=0)
        g = jnp.dot(pt, rhs, preferred_element_type=jnp.float32)
        g = pltpu.roll(g, 0, 1, stride=1, stride_axis=0)
        o_ref[0, k] = jnp.sum(g.reshape(per_dev, rows, lanes), axis=1)
        return carry

    lax.fori_loop(0, classes, body, 0)

def shift_scores(cube, refs, astep):
    n, radii, angles = cube.shape
    steps, classes = refs.shape[:2]
    turns = angles // astep
    x = cube.reshape(n, radii, turns, astep)
    x = jnp.roll(jnp.flip(x, axis=2), 1, axis=2)
    pt = x.transpose(0, 2, 3, 1).reshape(n * turns, astep * radii)
    b = jnp.arange(angles, dtype=jnp.int32)[:, None]
    col = jnp.arange(astep * 128, dtype=jnp.int32)[None, :]
    sel = (b == astep * ((col % 128) % turns) + col // 128).astype(cube.dtype)
    flops = 2 * steps * classes * (n * turns * radii * astep * 128 + radii * angles * astep * 128)
    return pl.pallas_call(
        _scores_kernel,
        grid=(steps,),
        in_specs=[
            pl.BlockSpec((n * turns, radii * astep), lambda s: (0, 0)),
            pl.BlockSpec((angles, astep * 128), lambda s: (0, 0)),
            pl.BlockSpec((1, classes, radii, angles), lambda s: (s, 0, 0, 0)),
        ],
        out_specs=pl.BlockSpec((1, classes, n, 128), lambda s: (s, 0, 0, 0)),
        out_shape=jax.ShapeDtypeStruct((steps, classes, n, 128), jnp.float32),
        cost_estimate=pl.CostEstimate(flops=flops, transcendentals=0, bytes_accessed=pt.size * 2 + refs.size * 2 + steps * classes * n * 128 * 4),
    )(pt, sel, refs)[..., :turns]


def rotate_each(cube, shifts):
    src = jnp.arange(ANGLES, dtype=jnp.int32)
    dst = (src[None, :, None] + shifts[:, None, None]) % ANGLES
    perm = (dst == src[None, None, :]).astype(cube.dtype)
    out = jnp.einsum("iab,ibc->iac", cube, perm, preferred_element_type=jnp.float32)
    return out.astype(cube.dtype)


def per_device(particles, averages, prior_mass, group_ids, class_ids, rot_ids, weights, owners):
    per_dev = particles.shape[0]
    pixels = particles.shape[1]
    groups = lax.axis_size("cls")
    doms = lax.axis_size("dom")
    chunk = pixels // doms
    per_group = averages.shape[0]
    capacity = per_dev * 3 // 8
    slots = groups * capacity
    me_dom = lax.axis_index("dom")
    me_cls = lax.axis_index("cls")
    cube = particles.reshape(per_dev, RADII, ANGLES)
    scale = 1.0 / math.sqrt(pixels)

    send_img = []
    send_wts = []
    for step in range(STEPS):
        shifts = rot_ids[step] * ASTEP
        rotated = rotate_each(cube, shifts).reshape(per_dev, pixels)
        target = group_ids[step, :, 0]
        onehot_group = (target[:, None] == jnp.arange(groups, dtype=jnp.int32)[None, :]).astype(
            jnp.int32
        )
        rank = jnp.sum((jnp.cumsum(onehot_group, axis=0) - 1) * onehot_group, axis=1)
        slot_of = target * capacity + rank
        placing = (slot_of[None, :] == jnp.arange(slots, dtype=jnp.int32)[:, None]).astype(
            jnp.bfloat16
        )
        images = jnp.dot(placing, rotated, preferred_element_type=jnp.float32).astype(jnp.bfloat16)
        images = images.reshape(groups, capacity, doms, chunk).transpose(2, 0, 1, 3)
        send_img.append(images)
        class_hot = (
            class_ids[step][:, None] == jnp.arange(per_group, dtype=jnp.int32)[None, :]
        ).astype(jnp.bfloat16)
        weighted_hot = class_hot * weights[step][:, None]
        wts = jnp.dot(placing, weighted_hot, preferred_element_type=jnp.float32).astype(
            jnp.bfloat16
        )
        wts = jnp.broadcast_to(wts.reshape(1, groups, capacity, per_group), (doms, groups, capacity, per_group))
        send_wts.append(wts)
    send_img = jnp.stack(send_img, axis=2).reshape(doms * groups, STEPS, capacity, chunk)
    send_wts = jnp.stack(send_wts, axis=2).reshape(doms * groups, STEPS, capacity, per_group)
    got_img = lax.all_to_all(send_img, ("dom", "cls"), 0, 0, tiled=True)
    got_wts = lax.all_to_all(send_wts, ("dom", "cls"), 0, 0, tiled=True)
    totals = lax.dot_general(
        got_wts, got_img, (((0, 2), (0, 2)), ((1,), (1,))), preferred_element_type=jnp.float32
    )
    mass = jnp.sum(got_wts.astype(jnp.float32), axis=(0, 2))

    current = lax.dynamic_slice_in_dim(averages, me_dom * chunk, chunk, axis=1)
    ref_chunks = []
    for step in range(STEPS):
        current = (prior_mass[:, None] * current + totals[step]) / (prior_mass + mass[step])[:, None]
        piece = current.astype(jnp.bfloat16)
        piece = jnp.where(me_cls == owners[step], piece, jnp.zeros_like(piece))
        ref_chunks.append(piece)
    ref_chunks = lax.psum(jnp.stack(ref_chunks, axis=0), "cls")
    all_refs = lax.all_gather(ref_chunks, "dom", axis=0, tiled=False)
    all_refs = all_refs.transpose(1, 2, 0, 3).reshape(STEPS, per_group, pixels)
    final = lax.all_gather(current, "dom", axis=0, tiled=False)
    final = final.transpose(1, 0, 2).reshape(per_group, pixels)

    shifted = shift_scores(cube, all_refs.reshape(STEPS, per_group, RADII, ANGLES), ASTEP)
    scores = shifted.transpose(0, 2, 3, 1).reshape(STEPS, per_dev, ROT * per_group)
    return (scores * scale, final)


def solution(mesh):
    return jax.shard_map(
        per_device,
        mesh=mesh,
        in_specs=(
            P(("dom", "cls"), None),
            P("cls", None),
            P("cls"),
            P(None, ("dom", "cls"), None),
            P(None, ("dom", "cls")),
            P(None, ("dom", "cls")),
            P(None, ("dom", "cls")),
            P(),
        ),
        out_specs=(P(None, ("dom", "cls"), None), P("cls", None)),
        check_vma=False,
    )
```

```python
import math

import jax
import jax.numpy as jnp
from jax import lax
from jax.experimental import pallas as pl
from jax.experimental.pallas import tpu as pltpu
from jax.sharding import PartitionSpec as P

RADII = 128
ANGLES = 128
ROT = 64
STEPS = 4
ASTEP = 2


def _scores_kernel(pt_ref, sel_ref, r_ref, o_ref):
    classes = r_ref.shape[1]
    per_dev = o_ref.shape[2]
    lanes = o_ref.shape[3]
    pt = pt_ref[...]
    sel = sel_ref[...]
    rows = pt.shape[0] // per_dev
    parts = sel.shape[1] // lanes

    def body(k, carry):
        split = jnp.dot(r_ref[0, k], sel, preferred_element_type=jnp.float32).astype(pt.dtype)
        rhs = jnp.concatenate([split[:, e * lanes:(e + 1) * lanes] for e in range(parts)], axis=0)
        g = jnp.dot(pt, rhs, preferred_element_type=jnp.float32)
        g = pltpu.roll(g, 0, 1, stride=1, stride_axis=0)
        o_ref[0, k] = jnp.sum(g.reshape(per_dev, rows, lanes), axis=1)
        return carry

    lax.fori_loop(0, classes, body, 0)

def shift_scores(cube, refs, astep):
    n, radii, angles = cube.shape
    steps, classes = refs.shape[:2]
    turns = angles // astep
    x = cube.reshape(n, radii, turns, astep)
    x = jnp.roll(jnp.flip(x, axis=2), 1, axis=2)
    pt = x.transpose(0, 2, 3, 1).reshape(n * turns, astep * radii)
    b = jnp.arange(angles, dtype=jnp.int32)[:, None]
    col = jnp.arange(astep * 128, dtype=jnp.int32)[None, :]
    sel = (b == astep * ((col % 128) % turns) + col // 128).astype(cube.dtype)
    flops = 2 * steps * classes * (n * turns * radii * astep * 128 + radii * angles * astep * 128)
    return pl.pallas_call(
        _scores_kernel,
        grid=(steps,),
        in_specs=[
            pl.BlockSpec((n * turns, radii * astep), lambda s: (0, 0)),
            pl.BlockSpec((angles, astep * 128), lambda s: (0, 0)),
            pl.BlockSpec((1, classes, radii, angles), lambda s: (s, 0, 0, 0)),
        ],
        out_specs=pl.BlockSpec((1, classes, n, 128), lambda s: (s, 0, 0, 0)),
        out_shape=jax.ShapeDtypeStruct((steps, classes, n, 128), jnp.float32),
        cost_estimate=pl.CostEstimate(flops=flops, transcendentals=0, bytes_accessed=pt.size * 2 + refs.size * 2 + steps * classes * n * 128 * 4),
    )(pt, sel, refs)[..., :turns]


def rotate_each(cube, shifts):
    src = jnp.arange(ANGLES, dtype=jnp.int32)
    dst = (src[None, :, None] + shifts[:, None, None]) % ANGLES
    perm = (dst == src[None, None, :]).astype(cube.dtype)
    out = jnp.einsum("iab,ibc->iac", cube, perm, preferred_element_type=jnp.float32)
    return out.astype(cube.dtype)


def per_device(particles, averages, prior_mass, group_ids, class_ids, rot_ids, weights, owners):
    per_dev = particles.shape[0]
    pixels = particles.shape[1]
    groups = lax.axis_size("cls")
    doms = lax.axis_size("dom")
    chunk = pixels // doms
    per_group = averages.shape[0]
    capacity = per_dev * 3 // 8
    slots = groups * capacity
    me_dom = lax.axis_index("dom")
    me_cls = lax.axis_index("cls")
    cube = particles.reshape(per_dev, RADII, ANGLES)
    scale = 1.0 / math.sqrt(pixels)

    send_img = []
    send_wts = []
    for step in range(STEPS):
        shifts = rot_ids[step] * ASTEP
        rotated = rotate_each(cube, shifts).reshape(per_dev, pixels)
        target = group_ids[step, :, 0]
        onehot_group = (target[:, None] == jnp.arange(groups, dtype=jnp.int32)[None, :]).astype(
            jnp.int32
        )
        rank = jnp.sum((jnp.cumsum(onehot_group, axis=0) - 1) * onehot_group, axis=1)
        slot_of = target * capacity + rank
        placing = (slot_of[None, :] == jnp.arange(slots, dtype=jnp.int32)[:, None]).astype(
            jnp.bfloat16
        )
        images = jnp.dot(placing, rotated, preferred_element_type=jnp.float32).astype(jnp.bfloat16)
        images = images.reshape(groups, capacity, doms, chunk).transpose(2, 0, 1, 3)
        send_img.append(images)
        class_hot = (
            class_ids[step][:, None] == jnp.arange(per_group, dtype=jnp.int32)[None, :]
        ).astype(jnp.bfloat16)
        weighted_hot = class_hot * weights[step][:, None]
        wts = jnp.dot(placing, weighted_hot, preferred_element_type=jnp.float32).astype(
            jnp.bfloat16
        )
        wts = jnp.broadcast_to(wts.reshape(1, groups, capacity, per_group), (doms, groups, capacity, per_group))
        send_wts.append(wts)
    send_img = jnp.stack(send_img, axis=2).reshape(doms * groups, STEPS, capacity, chunk)
    send_wts = jnp.stack(send_wts, axis=2).reshape(doms * groups, STEPS, capacity, per_group)
    got_img = lax.all_to_all(send_img, ("dom", "cls"), 0, 0, tiled=True)
    got_wts = lax.all_to_all(send_wts, ("dom", "cls"), 0, 0, tiled=True)
    totals = lax.dot_general(
        got_wts, got_img, (((0, 2), (0, 2)), ((1,), (1,))), preferred_element_type=jnp.float32
    )
    mass = jnp.sum(got_wts.astype(jnp.float32), axis=(0, 2))

    current = lax.dynamic_slice_in_dim(averages, me_dom * chunk, chunk, axis=1)
    ref_chunks = []
    for step in range(STEPS):
        current = (prior_mass[:, None] * current + totals[step]) / (prior_mass + mass[step])[:, None]
        ref_chunks.append(current.astype(jnp.bfloat16))
    rows = chunk // ANGLES
    ref_chunks = jnp.stack(ref_chunks, axis=0).reshape(STEPS, per_group, groups, rows // groups * ANGLES)
    got_refs = lax.all_to_all(ref_chunks.transpose(2, 0, 1, 3), "cls", 0, 0, tiled=True)
    owner_hot = (owners[None, :] == jnp.arange(groups, dtype=jnp.int32)[:, None]).astype(jnp.bfloat16)
    mine = jnp.einsum("gs,gskp->skp", owner_hot, got_refs, preferred_element_type=jnp.float32)
    mine = mine.astype(jnp.bfloat16)
    all_refs = lax.all_gather(mine, ("dom", "cls"), axis=0, tiled=False)
    all_refs = all_refs.transpose(1, 2, 0, 3).reshape(STEPS, per_group, pixels)
    final = lax.all_gather(current, "dom", axis=0, tiled=False)
    final = final.transpose(1, 0, 2).reshape(per_group, pixels)

    shifted = shift_scores(cube, all_refs.reshape(STEPS, per_group, RADII, ANGLES), ASTEP)
    scores = shifted.transpose(0, 2, 3, 1).reshape(STEPS, per_dev, ROT * per_group)
    return (scores * scale, final)


def solution(mesh):
    return jax.shard_map(
        per_device,
        mesh=mesh,
        in_specs=(
            P(("dom", "cls"), None),
            P("cls", None),
            P("cls"),
            P(None, ("dom", "cls"), None),
            P(None, ("dom", "cls")),
            P(None, ("dom", "cls")),
            P(None, ("dom", "cls")),
            P(),
        ),
        out_specs=(P(None, ("dom", "cls"), None), P("cls", None)),
        check_vma=False,
    )
```

```python
import math

import jax
import jax.numpy as jnp
from jax import lax
from jax.experimental import pallas as pl
from jax.experimental.pallas import tpu as pltpu
from jax.sharding import PartitionSpec as P

RADII = 128
ANGLES = 128
ROT = 64
STEPS = 4
ASTEP = 2


def _scores_kernel(pt_ref, sel_ref, r_ref, o_ref):
    classes = r_ref.shape[1]
    per_dev = o_ref.shape[2]
    lanes = o_ref.shape[3]
    pt = pt_ref[...]
    sel = sel_ref[...]
    rows = pt.shape[0] // per_dev
    parts = sel.shape[1] // lanes

    def body(k, carry):
        split = jnp.dot(r_ref[0, k], sel, preferred_element_type=jnp.float32).astype(pt.dtype)
        rhs = jnp.concatenate([split[:, e * lanes:(e + 1) * lanes] for e in range(parts)], axis=0)
        g = jnp.dot(pt, rhs, preferred_element_type=jnp.float32)
        g = pltpu.roll(g, 0, 1, stride=1, stride_axis=0)
        o_ref[0, k] = jnp.sum(g.reshape(per_dev, rows, lanes), axis=1)
        return carry

    lax.fori_loop(0, classes, body, 0)

def shift_scores(cube, refs, astep):
    n, radii, angles = cube.shape
    steps, classes = refs.shape[:2]
    turns = angles // astep
    x = cube.reshape(n, radii, turns, astep)
    x = jnp.roll(jnp.flip(x, axis=2), 1, axis=2)
    pt = x.transpose(0, 2, 3, 1).reshape(n * turns, astep * radii)
    b = jnp.arange(angles, dtype=jnp.int32)[:, None]
    col = jnp.arange(astep * 128, dtype=jnp.int32)[None, :]
    sel = (b == astep * ((col % 128) % turns) + col // 128).astype(cube.dtype)
    flops = 2 * steps * classes * (n * turns * radii * astep * 128 + radii * angles * astep * 128)
    return pl.pallas_call(
        _scores_kernel,
        grid=(steps,),
        in_specs=[
            pl.BlockSpec((n * turns, radii * astep), lambda s: (0, 0)),
            pl.BlockSpec((angles, astep * 128), lambda s: (0, 0)),
            pl.BlockSpec((1, classes, radii, angles), lambda s: (s, 0, 0, 0)),
        ],
        out_specs=pl.BlockSpec((1, classes, n, 128), lambda s: (s, 0, 0, 0)),
        out_shape=jax.ShapeDtypeStruct((steps, classes, n, 128), jnp.float32),
        cost_estimate=pl.CostEstimate(flops=flops, transcendentals=0, bytes_accessed=pt.size * 2 + refs.size * 2 + steps * classes * n * 128 * 4),
    )(pt, sel, refs)[..., :turns]


def rotate_each(cube, shifts):
    src = jnp.arange(ANGLES, dtype=jnp.int32)
    dst = (src[None, :, None] + shifts[:, None, None]) % ANGLES
    perm = (dst == src[None, None, :]).astype(cube.dtype)
    out = jnp.einsum("iab,ibc->iac", cube, perm, preferred_element_type=jnp.float32)
    return out.astype(cube.dtype)


def per_device(particles, averages, prior_mass, group_ids, class_ids, rot_ids, weights, owners):
    per_dev = particles.shape[0]
    pixels = particles.shape[1]
    groups = lax.axis_size("cls")
    doms = lax.axis_size("dom")
    chunk = pixels // doms
    per_group = averages.shape[0]
    capacity = per_dev * 3 // 8
    slots = groups * capacity
    me_dom = lax.axis_index("dom")
    me_cls = lax.axis_index("cls")
    cube = particles.reshape(per_dev, RADII, ANGLES)
    scale = 1.0 / math.sqrt(pixels)

    send_img = []
    send_wts = []
    for step in range(STEPS):
        shifts = rot_ids[step] * ASTEP
        rotated = rotate_each(cube, shifts).reshape(per_dev, pixels)
        target = group_ids[step, :, 0]
        onehot_group = (target[:, None] == jnp.arange(groups, dtype=jnp.int32)[None, :]).astype(
            jnp.int32
        )
        rank = jnp.sum((jnp.cumsum(onehot_group, axis=0) - 1) * onehot_group, axis=1)
        slot_of = target * capacity + rank
        placing = (slot_of[None, :] == jnp.arange(slots, dtype=jnp.int32)[:, None]).astype(
            jnp.bfloat16
        )
        images = jnp.dot(placing, rotated, preferred_element_type=jnp.float32).astype(jnp.bfloat16)
        images = images.reshape(groups, capacity, doms, chunk).transpose(2, 0, 1, 3)
        send_img.append(images)
        class_hot = (
            class_ids[step][:, None] == jnp.arange(per_group, dtype=jnp.int32)[None, :]
        ).astype(jnp.bfloat16)
        weighted_hot = class_hot * weights[step][:, None]
        wts = jnp.dot(placing, weighted_hot, preferred_element_type=jnp.float32).astype(
            jnp.bfloat16
        )
        wts = jnp.broadcast_to(wts.reshape(1, groups, capacity, per_group), (doms, groups, capacity, per_group))
        send_wts.append(wts)
    send_img = jnp.stack(send_img, axis=2).reshape(doms * groups, STEPS, capacity, chunk)
    send_wts = jnp.stack(send_wts, axis=2).reshape(doms * groups, STEPS, capacity, per_group)
    got_img = lax.all_to_all(send_img, ("dom", "cls"), 0, 0, tiled=True)
    got_wts = lax.all_to_all(send_wts, ("dom", "cls"), 0, 0, tiled=True)
    totals = lax.dot_general(
        got_wts, got_img, (((0, 2), (0, 2)), ((1,), (1,))), preferred_element_type=jnp.float32
    )
    mass = jnp.sum(got_wts.astype(jnp.float32), axis=(0, 2))

    current = lax.dynamic_slice_in_dim(averages, me_dom * chunk, chunk, axis=1)
    ref_chunks = []
    for step in range(STEPS):
        current = (prior_mass[:, None] * current + totals[step]) / (prior_mass + mass[step])[:, None]
        ref_chunks.append(current.astype(jnp.bfloat16))
    rows = chunk // ANGLES
    ref_chunks = jnp.stack(ref_chunks, axis=0).reshape(STEPS, per_group, groups, rows // groups * ANGLES)
    got_refs = lax.all_to_all(ref_chunks.transpose(2, 0, 1, 3), "cls", 0, 0, tiled=True)
    owner_hot = (owners[None, :] == jnp.arange(groups, dtype=jnp.int32)[:, None]).astype(jnp.bfloat16)
    mine = jnp.einsum("gs,gskp->skp", owner_hot, got_refs, preferred_element_type=jnp.float32)
    mine = mine.astype(jnp.bfloat16)
    owner_chunk = lax.all_gather(mine, "cls", axis=0, tiled=False)
    all_refs = lax.all_gather(owner_chunk, "dom", axis=0, tiled=False)
    all_refs = all_refs.transpose(2, 3, 0, 1, 4).reshape(STEPS, per_group, pixels)
    final = lax.all_gather(current, "dom", axis=0, tiled=False)
    final = final.transpose(1, 0, 2).reshape(per_group, pixels)

    shifted = shift_scores(cube, all_refs.reshape(STEPS, per_group, RADII, ANGLES), ASTEP)
    scores = shifted.transpose(0, 2, 3, 1).reshape(STEPS, per_dev, ROT * per_group)
    return (scores * scale, final)


def solution(mesh):
    return jax.shard_map(
        per_device,
        mesh=mesh,
        in_specs=(
            P(("dom", "cls"), None),
            P("cls", None),
            P("cls"),
            P(None, ("dom", "cls"), None),
            P(None, ("dom", "cls")),
            P(None, ("dom", "cls")),
            P(None, ("dom", "cls")),
            P(),
        ),
        out_specs=(P(None, ("dom", "cls"), None), P("cls", None)),
        check_vma=False,
    )
```

```python
import math

import jax
import jax.numpy as jnp
from jax import lax
from jax.experimental import pallas as pl
from jax.experimental.pallas import tpu as pltpu
from jax.sharding import PartitionSpec as P

RADII = 128
ANGLES = 128
ROT = 64
STEPS = 4
ASTEP = 2


def _scores_kernel(pt_ref, sel_ref, r_ref, o_ref):
    classes = r_ref.shape[1]
    per_dev = o_ref.shape[2]
    lanes = o_ref.shape[3]
    parts = pt_ref.shape[0]
    pt = jnp.concatenate([pt_ref[e] for e in range(parts)], axis=1)
    sel = sel_ref[...]
    rows = pt.shape[0] // per_dev

    def body(k, carry):
        split = jnp.dot(r_ref[0, k], sel, preferred_element_type=jnp.float32).astype(pt.dtype)
        rhs = jnp.concatenate([split[:, e * lanes:(e + 1) * lanes] for e in range(parts)], axis=0)
        g = jnp.dot(pt, rhs, preferred_element_type=jnp.float32)
        g = pltpu.roll(g, 0, 1, stride=1, stride_axis=0)
        o_ref[0, k] = jnp.sum(g.reshape(per_dev, rows, lanes), axis=1)
        return carry

    lax.fori_loop(0, classes, body, 0)


def shift_scores(cube, refs, astep):
    n, radii, angles = cube.shape
    steps, classes = refs.shape[:2]
    turns = angles // astep
    b = jnp.arange(angles, dtype=jnp.int32)[None, None, :]
    e = jnp.arange(astep, dtype=jnp.int32)[:, None, None]
    m = jnp.arange(turns, dtype=jnp.int32)[None, :, None]
    pick = (b == astep * ((turns - m) % turns) + e).astype(cube.dtype)
    pt = jnp.einsum("emb,iab->eima", pick, cube, preferred_element_type=jnp.float32)
    pt = pt.astype(cube.dtype).reshape(astep, n * turns, radii)
    b = jnp.arange(angles, dtype=jnp.int32)[:, None]
    col = jnp.arange(astep * 128, dtype=jnp.int32)[None, :]
    sel = (b == astep * ((col % 128) % turns) + col // 128).astype(cube.dtype)
    flops = 2 * steps * classes * (n * turns * radii * astep * 128 + radii * angles * astep * 128)
    return pl.pallas_call(
        _scores_kernel,
        grid=(steps,),
        in_specs=[
            pl.BlockSpec((astep, n * turns, radii), lambda s: (0, 0, 0)),
            pl.BlockSpec((angles, astep * 128), lambda s: (0, 0)),
            pl.BlockSpec((1, classes, radii, angles), lambda s: (s, 0, 0, 0)),
        ],
        out_specs=pl.BlockSpec((1, classes, n, 128), lambda s: (s, 0, 0, 0)),
        out_shape=jax.ShapeDtypeStruct((steps, classes, n, 128), jnp.float32),
        cost_estimate=pl.CostEstimate(flops=flops, transcendentals=0, bytes_accessed=pt.size * 2 + refs.size * 2 + steps * classes * n * 128 * 4),
    )(pt, sel, refs)[..., :turns]


def rotate_each(cube, shifts):
    src = jnp.arange(ANGLES, dtype=jnp.int32)
    dst = (src[None, :, None] + shifts[:, None, None]) % ANGLES
    perm = (dst == src[None, None, :]).astype(cube.dtype)
    out = jnp.einsum("iab,ibc->iac", cube, perm, preferred_element_type=jnp.float32)
    return out.astype(cube.dtype)


def per_device(particles, averages, prior_mass, group_ids, class_ids, rot_ids, weights, owners):
    per_dev = particles.shape[0]
    pixels = particles.shape[1]
    groups = lax.axis_size("cls")
    doms = lax.axis_size("dom")
    chunk = pixels // doms
    per_group = averages.shape[0]
    capacity = per_dev * 3 // 8
    slots = groups * capacity
    me_dom = lax.axis_index("dom")
    me_cls = lax.axis_index("cls")
    cube = particles.reshape(per_dev, RADII, ANGLES)
    scale = 1.0 / math.sqrt(pixels)

    send_img = []
    send_wts = []
    for step in range(STEPS):
        shifts = rot_ids[step] * ASTEP
        rotated = rotate_each(cube, shifts).reshape(per_dev, pixels)
        target = group_ids[step, :, 0]
        onehot_group = (target[:, None] == jnp.arange(groups, dtype=jnp.int32)[None, :]).astype(
            jnp.int32
        )
        rank = jnp.sum((jnp.cumsum(onehot_group, axis=0) - 1) * onehot_group, axis=1)
        slot_of = target * capacity + rank
        placing = (slot_of[None, :] == jnp.arange(slots, dtype=jnp.int32)[:, None]).astype(
            jnp.bfloat16
        )
        images = jnp.dot(placing, rotated, preferred_element_type=jnp.float32).astype(jnp.bfloat16)
        images = images.reshape(groups, capacity, doms, chunk).transpose(2, 0, 1, 3)
        send_img.append(images)
        class_hot = (
            class_ids[step][:, None] == jnp.arange(per_group, dtype=jnp.int32)[None, :]
        ).astype(jnp.bfloat16)
        weighted_hot = class_hot * weights[step][:, None]
        wts = jnp.dot(placing, weighted_hot, preferred_element_type=jnp.float32).astype(
            jnp.bfloat16
        )
        wts = jnp.broadcast_to(wts.reshape(1, groups, capacity, per_group), (doms, groups, capacity, per_group))
        send_wts.append(wts)
    send_img = jnp.stack(send_img, axis=2).reshape(doms * groups, STEPS, capacity, chunk)
    send_wts = jnp.stack(send_wts, axis=2).reshape(doms * groups, STEPS, capacity, per_group)
    got_img = lax.all_to_all(send_img, ("dom", "cls"), 0, 0, tiled=True)
    got_wts = lax.all_to_all(send_wts, ("dom", "cls"), 0, 0, tiled=True)
    totals = lax.dot_general(
        got_wts, got_img, (((0, 2), (0, 2)), ((1,), (1,))), preferred_element_type=jnp.float32
    )
    mass = jnp.sum(got_wts.astype(jnp.float32), axis=(0, 2))

    current = lax.dynamic_slice_in_dim(averages, me_dom * chunk, chunk, axis=1)
    ref_chunks = []
    for step in range(STEPS):
        current = (prior_mass[:, None] * current + totals[step]) / (prior_mass + mass[step])[:, None]
        ref_chunks.append(current.astype(jnp.bfloat16))
    rows = chunk // ANGLES
    ref_chunks = jnp.stack(ref_chunks, axis=0).reshape(STEPS, per_group, groups, rows // groups * ANGLES)
    got_refs = lax.all_to_all(ref_chunks.transpose(2, 0, 1, 3), "cls", 0, 0, tiled=True)
    owner_hot = (owners[None, :] == jnp.arange(groups, dtype=jnp.int32)[:, None]).astype(jnp.bfloat16)
    mine = jnp.einsum("gs,gskp->skp", owner_hot, got_refs, preferred_element_type=jnp.float32)
    mine = mine.astype(jnp.bfloat16)
    owner_chunk = lax.all_gather(mine, "cls", axis=2, tiled=False)
    all_refs = lax.all_gather(owner_chunk, "dom", axis=2, tiled=False)
    all_refs = all_refs.reshape(STEPS, per_group, pixels)
    final = lax.all_gather(current, "dom", axis=0, tiled=False)
    final = final.transpose(1, 0, 2).reshape(per_group, pixels)

    shifted = shift_scores(cube, all_refs.reshape(STEPS, per_group, RADII, ANGLES), ASTEP)
    scores = shifted.transpose(0, 2, 3, 1).reshape(STEPS, per_dev, ROT * per_group)
    return (scores * scale, final)


def solution(mesh):
    return jax.shard_map(
        per_device,
        mesh=mesh,
        in_specs=(
            P(("dom", "cls"), None),
            P("cls", None),
            P("cls"),
            P(None, ("dom", "cls"), None),
            P(None, ("dom", "cls")),
            P(None, ("dom", "cls")),
            P(None, ("dom", "cls")),
            P(),
        ),
        out_specs=(P(None, ("dom", "cls"), None), P("cls", None)),
        check_vma=False,
    )
```

```python
import math

import jax
import jax.numpy as jnp
from jax import lax
from jax.experimental import pallas as pl
from jax.experimental.pallas import tpu as pltpu
from jax.sharding import PartitionSpec as P

RADII = 128
ANGLES = 128
ROT = 64
STEPS = 4
ASTEP = 2


def _scores_kernel(pt_ref, sel_ref, r_ref, o_ref):
    classes = r_ref.shape[1]
    per_dev = o_ref.shape[2]
    lanes = o_ref.shape[3]
    parts = pt_ref.shape[0]
    pt = jnp.concatenate([pt_ref[e] for e in range(parts)], axis=1)
    sel = sel_ref[...]
    rows = pt.shape[0] // per_dev

    def body(k, carry):
        split = jnp.dot(r_ref[0, k], sel, preferred_element_type=jnp.float32).astype(pt.dtype)
        rhs = jnp.concatenate([split[:, e * lanes:(e + 1) * lanes] for e in range(parts)], axis=0)
        g = jnp.dot(pt, rhs, preferred_element_type=jnp.float32)
        g = pltpu.roll(g, 0, 1, stride=1, stride_axis=0)
        o_ref[0, k] = jnp.sum(g.reshape(per_dev, rows, lanes), axis=1)
        return carry

    lax.fori_loop(0, classes, body, 0)


def scores_operands(cube, astep):
    n, radii, angles = cube.shape
    turns = angles // astep
    b = jnp.arange(angles, dtype=jnp.int32)[None, None, :]
    e = jnp.arange(astep, dtype=jnp.int32)[:, None, None]
    m = jnp.arange(turns, dtype=jnp.int32)[None, :, None]
    pick = (b == astep * ((turns - m) % turns) + e).astype(cube.dtype)
    pt = jnp.einsum("emb,iab->eima", pick, cube, preferred_element_type=jnp.float32)
    pt = pt.astype(cube.dtype).reshape(astep, n * turns, radii)
    b = jnp.arange(angles, dtype=jnp.int32)[:, None]
    col = jnp.arange(astep * 128, dtype=jnp.int32)[None, :]
    sel = (b == astep * ((col % 128) % turns) + col // 128).astype(cube.dtype)
    return pt, sel


def shift_scores(pt, sel, refs, n, turns):
    astep, rows, radii = pt.shape
    steps, classes, _, angles = refs.shape
    flops = 2 * steps * classes * (rows * radii * astep * 128 + radii * angles * astep * 128)
    return pl.pallas_call(
        _scores_kernel,
        grid=(steps,),
        in_specs=[
            pl.BlockSpec((astep, rows, radii), lambda s: (0, 0, 0)),
            pl.BlockSpec((angles, astep * 128), lambda s: (0, 0)),
            pl.BlockSpec((1, classes, radii, angles), lambda s: (s, 0, 0, 0)),
        ],
        out_specs=pl.BlockSpec((1, classes, n, 128), lambda s: (s, 0, 0, 0)),
        out_shape=jax.ShapeDtypeStruct((steps, classes, n, 128), jnp.float32),
        cost_estimate=pl.CostEstimate(flops=flops, transcendentals=0, bytes_accessed=pt.size * 2 + refs.size * 2 + steps * classes * n * 128 * 4),
    )(pt, sel, refs)[..., :turns]


def rotate_each(cube, shifts):
    src = jnp.arange(ANGLES, dtype=jnp.int32)
    dst = (src[None, :, None] + shifts[:, None, None]) % ANGLES
    perm = (dst == src[None, None, :]).astype(cube.dtype)
    out = jnp.einsum("iab,ibc->iac", cube, perm, preferred_element_type=jnp.float32)
    return out.astype(cube.dtype)


def per_device(particles, averages, prior_mass, group_ids, class_ids, rot_ids, weights, owners):
    per_dev = particles.shape[0]
    pixels = particles.shape[1]
    groups = lax.axis_size("cls")
    doms = lax.axis_size("dom")
    chunk = pixels // doms
    per_group = averages.shape[0]
    capacity = per_dev * 3 // 8
    slots = groups * capacity
    me_dom = lax.axis_index("dom")
    me_cls = lax.axis_index("cls")
    cube = particles.reshape(per_dev, RADII, ANGLES)
    scale = 1.0 / math.sqrt(pixels)

    pt, sel = scores_operands(cube, ASTEP)
    rows = chunk // ANGLES
    current = lax.dynamic_slice_in_dim(averages, me_dom * chunk, chunk, axis=1)
    owner_hot = (owners[None, :] == jnp.arange(groups, dtype=jnp.int32)[:, None]).astype(jnp.bfloat16)
    all_scores = []
    for step in range(STEPS):
        shifts = rot_ids[step] * ASTEP
        rotated = rotate_each(cube, shifts).reshape(per_dev, pixels)
        target = group_ids[step, :, 0]
        onehot_group = (target[:, None] == jnp.arange(groups, dtype=jnp.int32)[None, :]).astype(
            jnp.int32
        )
        rank = jnp.sum((jnp.cumsum(onehot_group, axis=0) - 1) * onehot_group, axis=1)
        slot_of = target * capacity + rank
        placing = (slot_of[None, :] == jnp.arange(slots, dtype=jnp.int32)[:, None]).astype(
            jnp.bfloat16
        )
        images = jnp.dot(placing, rotated, preferred_element_type=jnp.float32).astype(jnp.bfloat16)
        images = images.reshape(groups, capacity, doms, chunk).transpose(2, 0, 1, 3)
        images = images.reshape(doms * groups, capacity, chunk)
        class_hot = (
            class_ids[step][:, None] == jnp.arange(per_group, dtype=jnp.int32)[None, :]
        ).astype(jnp.bfloat16)
        weighted_hot = class_hot * weights[step][:, None]
        wts = jnp.dot(placing, weighted_hot, preferred_element_type=jnp.float32).astype(
            jnp.bfloat16
        )
        wts = jnp.broadcast_to(wts.reshape(1, groups, capacity, per_group), (doms, groups, capacity, per_group))
        wts = wts.reshape(doms * groups, capacity, per_group)
        got_img = lax.all_to_all(images, ("dom", "cls"), 0, 0, tiled=True)
        got_wts = lax.all_to_all(wts, ("dom", "cls"), 0, 0, tiled=True)
        totals = lax.dot_general(
            got_wts, got_img, (((0, 1), (0, 1)), ((), ())), preferred_element_type=jnp.float32
        )
        mass = jnp.sum(got_wts.astype(jnp.float32), axis=(0, 1))
        current = (prior_mass[:, None] * current + totals) / (prior_mass + mass)[:, None]
        piece = current.astype(jnp.bfloat16).reshape(per_group, groups, rows // groups * ANGLES)
        got_refs = lax.all_to_all(piece.transpose(1, 0, 2), "cls", 0, 0, tiled=True)
        mine = jnp.einsum("g,gkp->kp", owner_hot[:, step], got_refs, preferred_element_type=jnp.float32)
        mine = mine.astype(jnp.bfloat16)
        owner_chunk = lax.all_gather(mine, "cls", axis=1, tiled=False)
        refs = lax.all_gather(owner_chunk, "dom", axis=1, tiled=False)
        refs = refs.reshape(1, per_group, RADII, ANGLES)
        all_scores.append(shift_scores(pt, sel, refs, per_dev, ROT)[0])
    current, _ = lax.optimization_barrier((current, refs))
    final = lax.all_gather(current, "dom", axis=0, tiled=False)
    final = final.transpose(1, 0, 2).reshape(per_group, pixels)
    scores = jnp.stack(all_scores, axis=0).transpose(0, 2, 3, 1).reshape(STEPS, per_dev, ROT * per_group)
    return (scores * scale, final)


def solution(mesh):
    return jax.shard_map(
        per_device,
        mesh=mesh,
        in_specs=(
            P(("dom", "cls"), None),
            P("cls", None),
            P("cls"),
            P(None, ("dom", "cls"), None),
            P(None, ("dom", "cls")),
            P(None, ("dom", "cls")),
            P(None, ("dom", "cls")),
            P(),
        ),
        out_specs=(P(None, ("dom", "cls"), None), P("cls", None)),
        check_vma=False,
    )
```

```python
import math

import jax
import jax.numpy as jnp
from jax import lax
from jax.experimental import pallas as pl
from jax.experimental.pallas import tpu as pltpu
from jax.sharding import PartitionSpec as P

RADII = 128
ANGLES = 128
ROT = 64
STEPS = 4
ASTEP = 2


def _scores_kernel(pt_ref, sel_ref, r_ref, o_ref):
    classes = r_ref.shape[1]
    per_dev = o_ref.shape[2]
    lanes = o_ref.shape[3]
    parts = pt_ref.shape[0]
    pt = jnp.concatenate([pt_ref[e] for e in range(parts)], axis=1)
    sel = sel_ref[...]
    rows = pt.shape[0] // per_dev

    def body(k, carry):
        split = jnp.dot(r_ref[0, k], sel, preferred_element_type=jnp.float32).astype(pt.dtype)
        rhs = jnp.concatenate([split[:, e * lanes:(e + 1) * lanes] for e in range(parts)], axis=0)
        g = jnp.dot(pt, rhs, preferred_element_type=jnp.float32)
        g = pltpu.roll(g, 0, 1, stride=1, stride_axis=0)
        o_ref[0, k] = jnp.sum(g.reshape(per_dev, rows, lanes), axis=1)
        return carry

    lax.fori_loop(0, classes, body, 0)


def shift_scores(cube, refs, astep):
    n, radii, angles = cube.shape
    steps, classes = refs.shape[:2]
    turns = angles // astep
    b = jnp.arange(angles, dtype=jnp.int32)[None, None, :]
    e = jnp.arange(astep, dtype=jnp.int32)[:, None, None]
    m = jnp.arange(turns, dtype=jnp.int32)[None, :, None]
    pick = (b == astep * ((turns - m) % turns) + e).astype(cube.dtype)
    pt = jnp.einsum("emb,iab->eima", pick, cube, preferred_element_type=jnp.float32)
    pt = pt.astype(cube.dtype).reshape(astep, n * turns, radii)
    b = jnp.arange(angles, dtype=jnp.int32)[:, None]
    col = jnp.arange(astep * 128, dtype=jnp.int32)[None, :]
    sel = (b == astep * ((col % 128) % turns) + col // 128).astype(cube.dtype)
    flops = 2 * steps * classes * (n * turns * radii * astep * 128 + radii * angles * astep * 128)
    return pl.pallas_call(
        _scores_kernel,
        grid=(steps,),
        in_specs=[
            pl.BlockSpec((astep, n * turns, radii), lambda s: (0, 0, 0)),
            pl.BlockSpec((angles, astep * 128), lambda s: (0, 0)),
            pl.BlockSpec((1, classes, radii, angles), lambda s: (s, 0, 0, 0)),
        ],
        out_specs=pl.BlockSpec((1, classes, n, 128), lambda s: (s, 0, 0, 0)),
        out_shape=jax.ShapeDtypeStruct((steps, classes, n, 128), jnp.float32),
        cost_estimate=pl.CostEstimate(flops=flops, transcendentals=0, bytes_accessed=pt.size * 2 + refs.size * 2 + steps * classes * n * 128 * 4),
    )(pt, sel, refs)[..., :turns]


def rotate_each(cube, shifts):
    src = jnp.arange(ANGLES, dtype=jnp.int32)
    dst = (src[None, :, None] + shifts[:, None, None]) % ANGLES
    perm = (dst == src[None, None, :]).astype(cube.dtype)
    out = jnp.einsum("iab,ibc->iac", cube, perm, preferred_element_type=jnp.float32)
    return out.astype(cube.dtype)


def per_device(particles, averages, prior_mass, group_ids, class_ids, rot_ids, weights, owners):
    per_dev = particles.shape[0]
    pixels = particles.shape[1]
    groups = lax.axis_size("cls")
    doms = lax.axis_size("dom")
    chunk = pixels // doms
    per_group = averages.shape[0]
    capacity = per_dev * 3 // 8
    slots = groups * capacity
    me_dom = lax.axis_index("dom")
    me_cls = lax.axis_index("cls")
    cube = particles.reshape(per_dev, RADII, ANGLES)
    scale = 1.0 / math.sqrt(pixels)

    send_img = []
    send_wts = []
    for step in range(STEPS):
        shifts = rot_ids[step] * ASTEP
        rotated = rotate_each(cube, shifts).reshape(per_dev, pixels)
        target = group_ids[step, :, 0]
        onehot_group = (target[:, None] == jnp.arange(groups, dtype=jnp.int32)[None, :]).astype(
            jnp.int32
        )
        rank = jnp.sum((jnp.cumsum(onehot_group, axis=0) - 1) * onehot_group, axis=1)
        slot_of = target * capacity + rank
        placing = (slot_of[None, :] == jnp.arange(slots, dtype=jnp.int32)[:, None]).astype(
            jnp.bfloat16
        )
        images = jnp.dot(placing, rotated, preferred_element_type=jnp.float32).astype(jnp.bfloat16)
        images = images.reshape(groups, capacity, doms, chunk).transpose(2, 0, 1, 3)
        send_img.append(images)
        class_hot = (
            class_ids[step][:, None] == jnp.arange(per_group, dtype=jnp.int32)[None, :]
        ).astype(jnp.bfloat16)
        weighted_hot = class_hot * weights[step][:, None]
        wts = jnp.dot(placing, weighted_hot, preferred_element_type=jnp.float32).astype(
            jnp.bfloat16
        )
        wts = jnp.broadcast_to(wts.reshape(1, groups, capacity, per_group), (doms, groups, capacity, per_group))
        send_wts.append(wts)
    send_img = jnp.stack(send_img, axis=2).reshape(doms * groups, STEPS, capacity, chunk)
    send_wts = jnp.stack(send_wts, axis=2).reshape(doms * groups, STEPS, capacity, per_group)
    got_img = lax.all_to_all(send_img, ("dom", "cls"), 0, 0, tiled=True)
    got_wts = lax.all_to_all(send_wts, ("dom", "cls"), 0, 0, tiled=True)
    totals = lax.dot_general(
        got_wts, got_img, (((0, 2), (0, 2)), ((1,), (1,))), preferred_element_type=jnp.float32
    )
    mass = jnp.sum(got_wts.astype(jnp.float32), axis=(0, 2))

    current = lax.dynamic_slice_in_dim(averages, me_dom * chunk, chunk, axis=1)
    ref_chunks = []
    for step in range(STEPS):
        current = (prior_mass[:, None] * current + totals[step]) / (prior_mass + mass[step])[:, None]
        ref_chunks.append(current.astype(jnp.bfloat16))
    rows = chunk // ANGLES
    ref_chunks = jnp.stack(ref_chunks, axis=0).reshape(STEPS, per_group, groups, rows // groups * ANGLES)
    got_refs = lax.all_to_all(ref_chunks.transpose(2, 0, 1, 3), "cls", 0, 0, tiled=True)
    owner_hot = (owners[None, :] == jnp.arange(groups, dtype=jnp.int32)[:, None]).astype(jnp.bfloat16)
    mine = jnp.einsum("gs,gskp->skp", owner_hot, got_refs, preferred_element_type=jnp.float32)
    mine = mine.astype(jnp.bfloat16)
    owner_chunk = lax.all_gather(mine, "cls", axis=2, tiled=False)
    all_refs = lax.all_gather(owner_chunk, "dom", axis=2, tiled=False)
    all_refs = all_refs.reshape(STEPS, per_group, pixels)
    current, all_refs = lax.optimization_barrier((current, all_refs))
    final = lax.all_gather(current, "dom", axis=0, tiled=False)
    final = final.transpose(1, 0, 2).reshape(per_group, pixels)

    shifted = shift_scores(cube, all_refs.reshape(STEPS, per_group, RADII, ANGLES), ASTEP)
    scores = shifted.transpose(0, 2, 3, 1).reshape(STEPS, per_dev, ROT * per_group)
    return (scores * scale, final)


def solution(mesh):
    return jax.shard_map(
        per_device,
        mesh=mesh,
        in_specs=(
            P(("dom", "cls"), None),
            P("cls", None),
            P("cls"),
            P(None, ("dom", "cls"), None),
            P(None, ("dom", "cls")),
            P(None, ("dom", "cls")),
            P(None, ("dom", "cls")),
            P(),
        ),
        out_specs=(P(None, ("dom", "cls"), None), P("cls", None)),
        check_vma=False,
    )
```

```python
import math

import jax
import jax.numpy as jnp
from jax import lax
from jax.experimental import pallas as pl
from jax.experimental.pallas import tpu as pltpu
from jax.sharding import PartitionSpec as P

RADII = 128
ANGLES = 128
ROT = 64
STEPS = 4
ASTEP = 2


def _scores_kernel(pt_ref, sel_ref, r_ref, o_ref, split_ref):
    classes = r_ref.shape[1]
    radii = r_ref.shape[2]
    per_dev = o_ref.shape[2]
    lanes = o_ref.shape[3]
    parts = pt_ref.shape[0]
    pt = jnp.concatenate([pt_ref[e] for e in range(parts)], axis=1)
    rows = pt.shape[0] // per_dev
    r_all = r_ref[0].reshape(classes * radii, r_ref.shape[3])
    split_ref[...] = jnp.dot(r_all, sel_ref[...], preferred_element_type=jnp.float32).astype(split_ref.dtype)

    def body(j, carry):
        halves = []
        for h in range(2):
            base = pl.multiple_of((2 * j + h) * radii, radii)
            blk = split_ref[pl.ds(base, radii), :]
            halves.append(jnp.concatenate([blk[:, e * lanes:(e + 1) * lanes] for e in range(parts)], axis=0))
        rhs = jnp.concatenate(halves, axis=1)
        g = jnp.dot(pt, rhs, preferred_element_type=jnp.float32)
        for h in range(2):
            gh = pltpu.roll(g[:, h * lanes:(h + 1) * lanes], 0, 1, stride=1, stride_axis=0)
            o_ref[0, 2 * j + h] = jnp.sum(gh.reshape(per_dev, rows, lanes), axis=1)
        return carry

    lax.fori_loop(0, classes // 2, body, 0)

def shift_scores(cube, refs, astep):
    n, radii, angles = cube.shape
    steps, classes = refs.shape[:2]
    turns = angles // astep
    b = jnp.arange(angles, dtype=jnp.int32)[None, None, :]
    e = jnp.arange(astep, dtype=jnp.int32)[:, None, None]
    m = jnp.arange(turns, dtype=jnp.int32)[None, :, None]
    pick = (b == astep * ((turns - m) % turns) + e).astype(cube.dtype)
    pt = jnp.einsum("emb,iab->eima", pick, cube, preferred_element_type=jnp.float32)
    pt = pt.astype(cube.dtype).reshape(astep, n * turns, radii)
    b = jnp.arange(angles, dtype=jnp.int32)[:, None]
    col = jnp.arange(astep * 128, dtype=jnp.int32)[None, :]
    sel = (b == astep * ((col % 128) % turns) + col // 128).astype(cube.dtype)
    flops = 2 * steps * classes * (n * turns * radii * astep * 128 + radii * angles * astep * 128)
    return pl.pallas_call(
        _scores_kernel,
        grid=(steps,),
        in_specs=[
            pl.BlockSpec((astep, n * turns, radii), lambda s: (0, 0, 0)),
            pl.BlockSpec((angles, astep * 128), lambda s: (0, 0)),
            pl.BlockSpec((1, classes, radii, angles), lambda s: (s, 0, 0, 0)),
        ],
        out_specs=pl.BlockSpec((1, classes, n, 128), lambda s: (s, 0, 0, 0)),
        out_shape=jax.ShapeDtypeStruct((steps, classes, n, 128), jnp.float32),
        scratch_shapes=[pltpu.VMEM((classes * radii, astep * 128), cube.dtype)],
        cost_estimate=pl.CostEstimate(flops=flops, transcendentals=0, bytes_accessed=pt.size * 2 + refs.size * 2 + steps * classes * n * 128 * 4),
    )(pt, sel, refs)[..., :turns]


def rotate_each(cube, shifts):
    src = jnp.arange(ANGLES, dtype=jnp.int32)
    dst = (src[None, :, None] + shifts[:, None, None]) % ANGLES
    perm = (dst == src[None, None, :]).astype(cube.dtype)
    out = jnp.einsum("iab,ibc->iac", cube, perm, preferred_element_type=jnp.float32)
    return out.astype(cube.dtype)


def per_device(particles, averages, prior_mass, group_ids, class_ids, rot_ids, weights, owners):
    per_dev = particles.shape[0]
    pixels = particles.shape[1]
    groups = lax.axis_size("cls")
    doms = lax.axis_size("dom")
    chunk = pixels // doms
    per_group = averages.shape[0]
    capacity = per_dev * 3 // 8
    slots = groups * capacity
    me_dom = lax.axis_index("dom")
    me_cls = lax.axis_index("cls")
    cube = particles.reshape(per_dev, RADII, ANGLES)
    scale = 1.0 / math.sqrt(pixels)

    send_img = []
    send_wts = []
    for step in range(STEPS):
        shifts = rot_ids[step] * ASTEP
        rotated = rotate_each(cube, shifts).reshape(per_dev, pixels)
        target = group_ids[step, :, 0]
        onehot_group = (target[:, None] == jnp.arange(groups, dtype=jnp.int32)[None, :]).astype(
            jnp.int32
        )
        rank = jnp.sum((jnp.cumsum(onehot_group, axis=0) - 1) * onehot_group, axis=1)
        slot_of = target * capacity + rank
        placing = (slot_of[None, :] == jnp.arange(slots, dtype=jnp.int32)[:, None]).astype(
            jnp.bfloat16
        )
        images = jnp.dot(placing, rotated, preferred_element_type=jnp.float32).astype(jnp.bfloat16)
        images = images.reshape(groups, capacity, doms, chunk).transpose(2, 0, 1, 3)
        send_img.append(images)
        class_hot = (
            class_ids[step][:, None] == jnp.arange(per_group, dtype=jnp.int32)[None, :]
        ).astype(jnp.bfloat16)
        weighted_hot = class_hot * weights[step][:, None]
        wts = jnp.dot(placing, weighted_hot, preferred_element_type=jnp.float32).astype(
            jnp.bfloat16
        )
        wts = jnp.broadcast_to(wts.reshape(1, groups, capacity, per_group), (doms, groups, capacity, per_group))
        send_wts.append(wts)
    send_img = jnp.stack(send_img, axis=2).reshape(doms * groups, STEPS, capacity, chunk)
    send_wts = jnp.stack(send_wts, axis=2).reshape(doms * groups, STEPS, capacity, per_group)
    got_img = lax.all_to_all(send_img, ("dom", "cls"), 0, 0, tiled=True)
    got_wts = lax.all_to_all(send_wts, ("dom", "cls"), 0, 0, tiled=True)
    totals = lax.dot_general(
        got_wts, got_img, (((0, 2), (0, 2)), ((1,), (1,))), preferred_element_type=jnp.float32
    )
    mass = jnp.sum(got_wts.astype(jnp.float32), axis=(0, 2))

    current = lax.dynamic_slice_in_dim(averages, me_dom * chunk, chunk, axis=1)
    ref_chunks = []
    for step in range(STEPS):
        current = (prior_mass[:, None] * current + totals[step]) / (prior_mass + mass[step])[:, None]
        ref_chunks.append(current.astype(jnp.bfloat16))
    rows = chunk // ANGLES
    ref_chunks = jnp.stack(ref_chunks, axis=0).reshape(STEPS, per_group, groups, rows // groups * ANGLES)
    got_refs = lax.all_to_all(ref_chunks.transpose(2, 0, 1, 3), "cls", 0, 0, tiled=True)
    owner_hot = (owners[None, :] == jnp.arange(groups, dtype=jnp.int32)[:, None]).astype(jnp.bfloat16)
    mine = jnp.einsum("gs,gskp->skp", owner_hot, got_refs, preferred_element_type=jnp.float32)
    mine = mine.astype(jnp.bfloat16)
    owner_chunk = lax.all_gather(mine, "cls", axis=2, tiled=False)
    all_refs = lax.all_gather(owner_chunk, "dom", axis=2, tiled=False)
    all_refs = all_refs.reshape(STEPS, per_group, pixels)
    final = lax.all_gather(current, "dom", axis=0, tiled=False)
    final = final.transpose(1, 0, 2).reshape(per_group, pixels)

    shifted = shift_scores(cube, all_refs.reshape(STEPS, per_group, RADII, ANGLES), ASTEP)
    scores = shifted.transpose(0, 2, 3, 1).reshape(STEPS, per_dev, ROT * per_group)
    return (scores * scale, final)


def solution(mesh):
    return jax.shard_map(
        per_device,
        mesh=mesh,
        in_specs=(
            P(("dom", "cls"), None),
            P("cls", None),
            P("cls"),
            P(None, ("dom", "cls"), None),
            P(None, ("dom", "cls")),
            P(None, ("dom", "cls")),
            P(None, ("dom", "cls")),
            P(),
        ),
        out_specs=(P(None, ("dom", "cls"), None), P("cls", None)),
        check_vma=False,
    )
```

```python
import math

import jax
import jax.numpy as jnp
from jax import lax
from jax.experimental import pallas as pl
from jax.experimental.pallas import tpu as pltpu
from jax.sharding import PartitionSpec as P

RADII = 128
ANGLES = 128
ROT = 64
STEPS = 4
ASTEP = 2


def _scores_kernel(pt_ref, sel_ref, r_ref, o_ref, split_ref):
    classes = r_ref.shape[1]
    radii = r_ref.shape[2]
    per_dev = o_ref.shape[2]
    lanes = o_ref.shape[3]
    parts = pt_ref.shape[0]
    pt = jnp.concatenate([pt_ref[e] for e in range(parts)], axis=1)
    rows = pt.shape[0] // per_dev
    r_all = r_ref[0].reshape(classes * radii, r_ref.shape[3])
    split_ref[...] = jnp.dot(r_all, sel_ref[...], preferred_element_type=jnp.float32).astype(split_ref.dtype)

    def body(j, carry):
        halves = []
        for h in range(2):
            base = pl.multiple_of((2 * j + h) * radii, radii)
            blk = split_ref[pl.ds(base, radii), :]
            halves.append(jnp.concatenate([blk[:, e * lanes:(e + 1) * lanes] for e in range(parts)], axis=0))
        rhs = jnp.concatenate(halves, axis=1)
        g = jnp.dot(pt, rhs, preferred_element_type=jnp.float32)
        for h in range(2):
            gh = pltpu.roll(g[:, h * lanes:(h + 1) * lanes], 0, 1, stride=1, stride_axis=0)
            o_ref[0, 2 * j + h] = jnp.sum(gh.reshape(per_dev, rows, lanes), axis=1)
        return carry

    lax.fori_loop(0, classes // 2, body, 0)

def shift_scores(cube, refs, astep):
    n, radii, angles = cube.shape
    steps, classes = refs.shape[:2]
    turns = angles // astep
    b = jnp.arange(angles, dtype=jnp.int32)[None, None, :]
    e = jnp.arange(astep, dtype=jnp.int32)[:, None, None]
    m = jnp.arange(turns, dtype=jnp.int32)[None, :, None]
    pick = (b == astep * ((turns - m) % turns) + e).astype(cube.dtype)
    pt = jnp.einsum("emb,iab->eima", pick, cube, preferred_element_type=jnp.float32)
    pt = pt.astype(cube.dtype).reshape(astep, n * turns, radii)
    b = jnp.arange(angles, dtype=jnp.int32)[:, None]
    col = jnp.arange(astep * 128, dtype=jnp.int32)[None, :]
    sel = (b == astep * ((col % 128) % turns) + col // 128).astype(cube.dtype)
    flops = 2 * steps * classes * (n * turns * radii * astep * 128 + radii * angles * astep * 128)
    return pl.pallas_call(
        _scores_kernel,
        grid=(steps,),
        in_specs=[
            pl.BlockSpec((astep, n * turns, radii), lambda s: (0, 0, 0)),
            pl.BlockSpec((angles, astep * 128), lambda s: (0, 0)),
            pl.BlockSpec((1, classes, radii, angles), lambda s: (s, 0, 0, 0)),
        ],
        out_specs=pl.BlockSpec((1, classes, n, 128), lambda s: (s, 0, 0, 0)),
        out_shape=jax.ShapeDtypeStruct((steps, classes, n, 128), jnp.float32),
        scratch_shapes=[pltpu.VMEM((classes * radii, astep * 128), cube.dtype)],
        cost_estimate=pl.CostEstimate(flops=flops, transcendentals=0, bytes_accessed=pt.size * 2 + refs.size * 2 + steps * classes * n * 128 * 4),
    )(pt, sel, refs)[..., :turns]


def rotate_each(cube, shifts):
    src = jnp.arange(ANGLES, dtype=jnp.int32)
    dst = (src[None, :, None] + shifts[:, None, None]) % ANGLES
    perm = (dst == src[None, None, :]).astype(cube.dtype)
    out = jnp.einsum("iab,ibc->iac", cube, perm, preferred_element_type=jnp.float32)
    return out.astype(cube.dtype)


def per_device(particles, averages, prior_mass, group_ids, class_ids, rot_ids, weights, owners):
    per_dev = particles.shape[0]
    pixels = particles.shape[1]
    groups = lax.axis_size("cls")
    doms = lax.axis_size("dom")
    chunk = pixels // doms
    per_group = averages.shape[0]
    capacity = per_dev * 3 // 8
    slots = groups * capacity
    me_dom = lax.axis_index("dom")
    me_cls = lax.axis_index("cls")
    cube = particles.reshape(per_dev, RADII, ANGLES)
    scale = 1.0 / math.sqrt(pixels)

    send_img = []
    send_wts = []
    for step in range(STEPS):
        shifts = rot_ids[step] * ASTEP
        rotated = rotate_each(cube, shifts).reshape(per_dev, pixels)
        target = group_ids[step, :, 0]
        onehot_group = (target[:, None] == jnp.arange(groups, dtype=jnp.int32)[None, :]).astype(
            jnp.int32
        )
        rank = jnp.sum((jnp.cumsum(onehot_group, axis=0) - 1) * onehot_group, axis=1)
        slot_of = target * capacity + rank
        placing = (slot_of[None, :] == jnp.arange(slots, dtype=jnp.int32)[:, None]).astype(
            jnp.bfloat16
        )
        images = jnp.dot(placing, rotated, preferred_element_type=jnp.float32).astype(jnp.bfloat16)
        images = images.reshape(groups, capacity, doms, chunk).transpose(2, 0, 1, 3)
        send_img.append(images)
        class_hot = (
            class_ids[step][:, None] == jnp.arange(per_group, dtype=jnp.int32)[None, :]
        ).astype(jnp.bfloat16)
        weighted_hot = class_hot * weights[step][:, None]
        wts = jnp.dot(placing, weighted_hot, preferred_element_type=jnp.float32).astype(
            jnp.bfloat16
        )
        wts = jnp.broadcast_to(wts.reshape(1, groups, capacity, per_group), (doms, groups, capacity, per_group))
        send_wts.append(wts)
    send_img = jnp.stack(send_img, axis=2).reshape(doms * groups, STEPS, capacity, chunk)
    send_wts = jnp.stack(send_wts, axis=2).reshape(doms * groups, STEPS, capacity, per_group)
    got_img = lax.all_to_all(send_img, ("dom", "cls"), 0, 0, tiled=True)
    got_wts = lax.all_to_all(send_wts, ("dom", "cls"), 0, 0, tiled=True)
    totals = lax.dot_general(
        got_wts, got_img, (((0, 2), (0, 2)), ((1,), (1,))), preferred_element_type=jnp.float32
    )
    mass = jnp.sum(got_wts.astype(jnp.float32), axis=(0, 2))

    current = lax.dynamic_slice_in_dim(averages, me_dom * chunk, chunk, axis=1)
    ref_chunks = []
    for step in range(STEPS):
        current = (prior_mass[:, None] * current + totals[step]) / (prior_mass + mass[step])[:, None]
        ref_chunks.append(current.astype(jnp.bfloat16))
    ref_chunks = jnp.stack(ref_chunks, axis=0)
    ref_chunks = jnp.broadcast_to(ref_chunks[None], (groups,) + ref_chunks.shape)
    got_refs = lax.all_to_all(ref_chunks, "cls", 0, 0, tiled=True)
    owner_hot = (owners[None, :] == jnp.arange(groups, dtype=jnp.int32)[:, None]).astype(jnp.bfloat16)
    owner_chunk = jnp.einsum("gs,gskp->skp", owner_hot, got_refs, preferred_element_type=jnp.float32)
    owner_chunk = owner_chunk.astype(jnp.bfloat16)
    all_refs = lax.all_gather(owner_chunk, "dom", axis=2, tiled=False)
    all_refs = all_refs.reshape(STEPS, per_group, pixels)
    current = current + 0.0 * all_refs[0, 0, 0].astype(jnp.float32)
    final = lax.all_gather(current, "dom", axis=0, tiled=False)
    final = final.transpose(1, 0, 2).reshape(per_group, pixels)

    shifted = shift_scores(cube, all_refs.reshape(STEPS, per_group, RADII, ANGLES), ASTEP)
    scores = shifted.transpose(0, 2, 3, 1).reshape(STEPS, per_dev, ROT * per_group)
    return (scores * scale, final)


def solution(mesh):
    return jax.shard_map(
        per_device,
        mesh=mesh,
        in_specs=(
            P(("dom", "cls"), None),
            P("cls", None),
            P("cls"),
            P(None, ("dom", "cls"), None),
            P(None, ("dom", "cls")),
            P(None, ("dom", "cls")),
            P(None, ("dom", "cls")),
            P(),
        ),
        out_specs=(P(None, ("dom", "cls"), None), P("cls", None)),
        check_vma=False,
    )
```

```python
import math

import jax
import jax.numpy as jnp
from jax import lax
from jax.experimental import pallas as pl
from jax.experimental.pallas import tpu as pltpu
from jax.sharding import PartitionSpec as P

RADII = 128
ANGLES = 128
ROT = 64
STEPS = 4
ASTEP = 2


def _scores_kernel(pt_ref, sel_ref, r_ref, o_ref, split_ref):
    classes = r_ref.shape[1]
    radii = r_ref.shape[2]
    per_dev = o_ref.shape[2]
    lanes = o_ref.shape[3]
    parts = pt_ref.shape[0]
    pt = jnp.concatenate([pt_ref[e] for e in range(parts)], axis=1)
    rows = pt.shape[0] // per_dev
    r_all = r_ref[0].reshape(classes * radii, r_ref.shape[3])
    split_ref[...] = jnp.dot(r_all, sel_ref[...], preferred_element_type=jnp.float32).astype(split_ref.dtype)

    def body(j, carry):
        halves = []
        for h in range(2):
            base = pl.multiple_of((2 * j + h) * radii, radii)
            blk = split_ref[pl.ds(base, radii), :]
            halves.append(jnp.concatenate([blk[:, e * lanes:(e + 1) * lanes] for e in range(parts)], axis=0))
        rhs = jnp.concatenate(halves, axis=1)
        g = jnp.dot(pt, rhs, preferred_element_type=jnp.float32)
        for h in range(2):
            gh = pltpu.roll(g[:, h * lanes:(h + 1) * lanes], 0, 1, stride=1, stride_axis=0)
            o_ref[0, 2 * j + h] = jnp.sum(gh.reshape(per_dev, rows, lanes), axis=1)
        return carry

    lax.fori_loop(0, classes // 2, body, 0)

def shift_scores(cube, refs, astep):
    n, radii, angles = cube.shape
    steps, classes = refs.shape[:2]
    turns = angles // astep
    b = jnp.arange(angles, dtype=jnp.int32)[None, None, :]
    e = jnp.arange(astep, dtype=jnp.int32)[:, None, None]
    m = jnp.arange(turns, dtype=jnp.int32)[None, :, None]
    pick = (b == astep * ((turns - m) % turns) + e).astype(cube.dtype)
    pt = jnp.einsum("emb,iab->eima", pick, cube, preferred_element_type=jnp.float32)
    pt = pt.astype(cube.dtype).reshape(astep, n * turns, radii)
    b = jnp.arange(angles, dtype=jnp.int32)[:, None]
    col = jnp.arange(astep * 128, dtype=jnp.int32)[None, :]
    sel = (b == astep * ((col % 128) % turns) + col // 128).astype(cube.dtype)
    flops = 2 * steps * classes * (n * turns * radii * astep * 128 + radii * angles * astep * 128)
    return pl.pallas_call(
        _scores_kernel,
        grid=(steps,),
        in_specs=[
            pl.BlockSpec((astep, n * turns, radii), lambda s: (0, 0, 0)),
            pl.BlockSpec((angles, astep * 128), lambda s: (0, 0)),
            pl.BlockSpec((1, classes, radii, angles), lambda s: (s, 0, 0, 0)),
        ],
        out_specs=pl.BlockSpec((1, classes, n, 128), lambda s: (s, 0, 0, 0)),
        out_shape=jax.ShapeDtypeStruct((steps, classes, n, 128), jnp.float32),
        scratch_shapes=[pltpu.VMEM((classes * radii, astep * 128), cube.dtype)],
        cost_estimate=pl.CostEstimate(flops=flops, transcendentals=0, bytes_accessed=pt.size * 2 + refs.size * 2 + steps * classes * n * 128 * 4),
    )(pt, sel, refs)[..., :turns]


def rotate_each(cube, shifts):
    src = jnp.arange(ANGLES, dtype=jnp.int32)
    dst = (src[None, :, None] + shifts[:, None, None]) % ANGLES
    perm = (dst == src[None, None, :]).astype(cube.dtype)
    out = jnp.einsum("iab,ibc->iac", cube, perm, preferred_element_type=jnp.float32)
    return out.astype(cube.dtype)


def per_device(particles, averages, prior_mass, group_ids, class_ids, rot_ids, weights, owners):
    per_dev = particles.shape[0]
    pixels = particles.shape[1]
    groups = lax.axis_size("cls")
    doms = lax.axis_size("dom")
    chunk = pixels // doms
    per_group = averages.shape[0]
    capacity = per_dev * 3 // 8
    slots = groups * capacity
    me_dom = lax.axis_index("dom")
    me_cls = lax.axis_index("cls")
    cube = particles.reshape(per_dev, RADII, ANGLES)
    scale = 1.0 / math.sqrt(pixels)

    send_img = []
    send_wts = []
    for step in range(STEPS):
        shifts = rot_ids[step] * ASTEP
        rotated = rotate_each(cube, shifts).reshape(per_dev, pixels)
        target = group_ids[step, :, 0]
        onehot_group = (target[:, None] == jnp.arange(groups, dtype=jnp.int32)[None, :]).astype(
            jnp.int32
        )
        rank = jnp.sum((jnp.cumsum(onehot_group, axis=0) - 1) * onehot_group, axis=1)
        slot_of = target * capacity + rank
        placing = (slot_of[None, :] == jnp.arange(slots, dtype=jnp.int32)[:, None]).astype(
            jnp.bfloat16
        )
        images = jnp.dot(placing, rotated, preferred_element_type=jnp.float32).astype(jnp.bfloat16)
        images = images.reshape(groups, capacity, doms, chunk).transpose(2, 0, 1, 3)
        send_img.append(images)
        class_hot = (
            class_ids[step][:, None] == jnp.arange(per_group, dtype=jnp.int32)[None, :]
        ).astype(jnp.bfloat16)
        weighted_hot = class_hot * weights[step][:, None]
        wts = jnp.dot(placing, weighted_hot, preferred_element_type=jnp.float32).astype(
            jnp.bfloat16
        )
        wts = jnp.broadcast_to(wts.reshape(1, groups, capacity, per_group), (doms, groups, capacity, per_group))
        send_wts.append(wts)
    send_img = jnp.stack(send_img, axis=2).reshape(doms * groups, STEPS, capacity, chunk)
    send_wts = jnp.stack(send_wts, axis=2).reshape(doms * groups, STEPS, capacity, per_group)
    got_img = lax.all_to_all(send_img, ("dom", "cls"), 0, 0, tiled=True)
    got_wts = lax.all_to_all(send_wts, ("dom", "cls"), 0, 0, tiled=True)
    totals = lax.dot_general(
        got_wts, got_img, (((0, 2), (0, 2)), ((1,), (1,))), preferred_element_type=jnp.float32
    )
    mass = jnp.sum(got_wts.astype(jnp.float32), axis=(0, 2))

    current = lax.dynamic_slice_in_dim(averages, me_dom * chunk, chunk, axis=1)
    ref_chunks = []
    for step in range(STEPS):
        current = (prior_mass[:, None] * current + totals[step]) / (prior_mass + mass[step])[:, None]
        ref_chunks.append(current.astype(jnp.bfloat16))
    ref_chunks = jnp.stack(ref_chunks, axis=0).reshape(STEPS, per_group, chunk // ANGLES, ANGLES)
    ref_chunks = jnp.broadcast_to(ref_chunks[None], (groups,) + ref_chunks.shape)
    got_refs = lax.all_to_all(ref_chunks, "cls", 0, 0, tiled=True)
    owner_hot = (owners[None, :] == jnp.arange(groups, dtype=jnp.int32)[:, None]).astype(jnp.bfloat16)
    owner_chunk = jnp.einsum("gs,gskrc->skrc", owner_hot, got_refs, preferred_element_type=jnp.float32)
    owner_chunk = owner_chunk.astype(jnp.bfloat16)
    all_refs = lax.all_gather(owner_chunk, "dom", axis=2, tiled=False)
    all_refs = all_refs.reshape(STEPS, per_group, pixels)
    current = current + 0.0 * all_refs[0, 0, 0].astype(jnp.float32)
    final = lax.all_gather(current, "dom", axis=1, tiled=False).reshape(per_group, pixels)

    shifted = shift_scores(cube, all_refs.reshape(STEPS, per_group, RADII, ANGLES), ASTEP)
    scores = shifted.transpose(0, 2, 3, 1).reshape(STEPS, per_dev, ROT * per_group)
    return (scores * scale, final)


def solution(mesh):
    return jax.shard_map(
        per_device,
        mesh=mesh,
        in_specs=(
            P(("dom", "cls"), None),
            P("cls", None),
            P("cls"),
            P(None, ("dom", "cls"), None),
            P(None, ("dom", "cls")),
            P(None, ("dom", "cls")),
            P(None, ("dom", "cls")),
            P(),
        ),
        out_specs=(P(None, ("dom", "cls"), None), P("cls", None)),
        check_vma=False,
    )
```

```python
import math

import jax
import jax.numpy as jnp
from jax import lax
from jax.experimental import pallas as pl
from jax.experimental.pallas import tpu as pltpu
from jax.sharding import PartitionSpec as P

RADII = 128
ANGLES = 128
ROT = 64
STEPS = 4
ASTEP = 2


def _scores_kernel(pt_ref, sel_ref, r_ref, o_ref, split_ref):
    classes = r_ref.shape[1]
    radii = r_ref.shape[2]
    per_dev = o_ref.shape[2]
    lanes = o_ref.shape[3]
    parts = pt_ref.shape[0]
    pt = jnp.concatenate([pt_ref[e] for e in range(parts)], axis=1)
    rows = pt.shape[0] // per_dev
    r_all = r_ref[0].reshape(classes * radii, r_ref.shape[3])
    split_ref[...] = jnp.dot(r_all, sel_ref[...], preferred_element_type=jnp.float32).astype(split_ref.dtype)

    def body(j, carry):
        halves = []
        for h in range(2):
            base = pl.multiple_of((2 * j + h) * radii, radii)
            blk = split_ref[pl.ds(base, radii), :]
            halves.append(jnp.concatenate([blk[:, e * lanes:(e + 1) * lanes] for e in range(parts)], axis=0))
        rhs = jnp.concatenate(halves, axis=1)
        g = jnp.dot(pt, rhs, preferred_element_type=jnp.float32)
        for h in range(2):
            gh = pltpu.roll(g[:, h * lanes:(h + 1) * lanes], 0, 1, stride=1, stride_axis=0)
            o_ref[0, 2 * j + h] = jnp.sum(gh.reshape(per_dev, rows, lanes), axis=1)
        return carry

    lax.fori_loop(0, classes // 2, body, 0)

def shift_scores(cube, refs, astep):
    n, radii, angles = cube.shape
    steps, classes = refs.shape[:2]
    turns = angles // astep
    b = jnp.arange(angles, dtype=jnp.int32)[None, None, :]
    e = jnp.arange(astep, dtype=jnp.int32)[:, None, None]
    m = jnp.arange(turns, dtype=jnp.int32)[None, :, None]
    pick = (b == astep * ((turns - m) % turns) + e).astype(cube.dtype)
    pt = jnp.einsum("emb,iab->eima", pick, cube, preferred_element_type=jnp.float32)
    pt = pt.astype(cube.dtype).reshape(astep, n * turns, radii)
    b = jnp.arange(angles, dtype=jnp.int32)[:, None]
    col = jnp.arange(astep * 128, dtype=jnp.int32)[None, :]
    sel = (b == astep * ((col % 128) % turns) + col // 128).astype(cube.dtype)
    flops = 2 * steps * classes * (n * turns * radii * astep * 128 + radii * angles * astep * 128)
    return pl.pallas_call(
        _scores_kernel,
        grid=(steps,),
        in_specs=[
            pl.BlockSpec((astep, n * turns, radii), lambda s: (0, 0, 0)),
            pl.BlockSpec((angles, astep * 128), lambda s: (0, 0)),
            pl.BlockSpec((1, classes, radii, angles), lambda s: (s, 0, 0, 0)),
        ],
        out_specs=pl.BlockSpec((1, classes, n, 128), lambda s: (s, 0, 0, 0)),
        out_shape=jax.ShapeDtypeStruct((steps, classes, n, 128), jnp.float32),
        scratch_shapes=[pltpu.VMEM((classes * radii, astep * 128), cube.dtype)],
        cost_estimate=pl.CostEstimate(flops=flops, transcendentals=0, bytes_accessed=pt.size * 2 + refs.size * 2 + steps * classes * n * 128 * 4),
    )(pt, sel, refs)[..., :turns]


def rotate_each(cube, shifts):
    src = jnp.arange(ANGLES, dtype=jnp.int32)
    dst = (src[None, :, None] + shifts[:, None, None]) % ANGLES
    perm = (dst == src[None, None, :]).astype(cube.dtype)
    out = jnp.einsum("iab,ibc->iac", cube, perm, preferred_element_type=jnp.float32)
    return out.astype(cube.dtype)


def per_device(particles, averages, prior_mass, group_ids, class_ids, rot_ids, weights, owners):
    per_dev = particles.shape[0]
    pixels = particles.shape[1]
    groups = lax.axis_size("cls")
    doms = lax.axis_size("dom")
    chunk = pixels // doms
    per_group = averages.shape[0]
    capacity = per_dev * 3 // 8
    slots = groups * capacity
    me_dom = lax.axis_index("dom")
    me_cls = lax.axis_index("cls")
    cube = particles.reshape(per_dev, RADII, ANGLES)
    scale = 1.0 / math.sqrt(pixels)

    send_img = []
    for step in range(STEPS):
        shifts = rot_ids[step] * ASTEP
        rotated = rotate_each(cube, shifts).reshape(per_dev, pixels)
        target = group_ids[step, :, 0]
        onehot_group = (target[:, None] == jnp.arange(groups, dtype=jnp.int32)[None, :]).astype(
            jnp.int32
        )
        rank = jnp.sum((jnp.cumsum(onehot_group, axis=0) - 1) * onehot_group, axis=1)
        slot_of = target * capacity + rank
        placing = (slot_of[None, :] == jnp.arange(slots, dtype=jnp.int32)[:, None]).astype(
            jnp.bfloat16
        )
        images = jnp.dot(placing, rotated, preferred_element_type=jnp.float32).astype(jnp.bfloat16)
        images = images.reshape(groups, capacity, doms, chunk).transpose(2, 0, 1, 3)
        send_img.append(images)
    send_img = jnp.stack(send_img, axis=2).reshape(doms * groups, STEPS, capacity, chunk)
    got_img = lax.all_to_all(send_img, ("dom", "cls"), 0, 0, tiled=True)
    meta = jnp.stack(
        [group_ids[:, :, 0].astype(jnp.float32), class_ids.astype(jnp.float32), weights.astype(jnp.float32)]
    )
    meta = lax.all_gather(meta, ("dom", "cls"), axis=1, tiled=False)
    src_group = meta[0].astype(jnp.int32)
    src_class = meta[1].astype(jnp.int32)
    src_weight = meta[2].astype(jnp.bfloat16)
    hot = (src_group[..., None] == jnp.arange(groups, dtype=jnp.int32)).astype(jnp.int32)
    src_rank = jnp.sum((jnp.cumsum(hot, axis=2) - 1) * hot, axis=3)
    in_slot = (src_group == me_cls)[:, :, None, :] & (
        src_rank[:, :, None, :] == jnp.arange(capacity, dtype=jnp.int32)[None, None, :, None]
    )
    weighted_hot = (
        src_class[..., None] == jnp.arange(per_group, dtype=jnp.int32)
    ).astype(jnp.bfloat16) * src_weight[..., None]
    got_wts = jnp.einsum(
        "jsqp,jspk->jsqk", in_slot.astype(jnp.bfloat16), weighted_hot, preferred_element_type=jnp.float32
    ).astype(jnp.bfloat16)
    totals = lax.dot_general(
        got_wts, got_img, (((0, 2), (0, 2)), ((1,), (1,))), preferred_element_type=jnp.float32
    )
    mass = jnp.sum(got_wts.astype(jnp.float32), axis=(0, 2))

    current = lax.dynamic_slice_in_dim(averages, me_dom * chunk, chunk, axis=1)
    ref_chunks = []
    for step in range(STEPS):
        current = (prior_mass[:, None] * current + totals[step]) / (prior_mass + mass[step])[:, None]
        ref_chunks.append(current.astype(jnp.bfloat16))
    ref_chunks = jnp.stack(ref_chunks, axis=0)
    ref_chunks = jnp.broadcast_to(ref_chunks[None], (groups,) + ref_chunks.shape)
    got_refs = lax.all_to_all(ref_chunks, "cls", 0, 0, tiled=True)
    owner_hot = (owners[None, :] == jnp.arange(groups, dtype=jnp.int32)[:, None]).astype(jnp.bfloat16)
    owner_chunk = jnp.einsum("gs,gskp->skp", owner_hot, got_refs, preferred_element_type=jnp.float32)
    owner_chunk = owner_chunk.astype(jnp.bfloat16)
    all_refs = lax.all_gather(owner_chunk, "dom", axis=2, tiled=False)
    all_refs = all_refs.reshape(STEPS, per_group, pixels)
    current = current + 0.0 * all_refs[0, 0, 0].astype(jnp.float32)
    final = lax.all_gather(current, "dom", axis=0, tiled=False)
    final = final.transpose(1, 0, 2).reshape(per_group, pixels)

    shifted = shift_scores(cube, all_refs.reshape(STEPS, per_group, RADII, ANGLES), ASTEP)
    scores = shifted.transpose(0, 2, 3, 1).reshape(STEPS, per_dev, ROT * per_group)
    return (scores * scale, final)


def solution(mesh):
    return jax.shard_map(
        per_device,
        mesh=mesh,
        in_specs=(
            P(("dom", "cls"), None),
            P("cls", None),
            P("cls"),
            P(None, ("dom", "cls"), None),
            P(None, ("dom", "cls")),
            P(None, ("dom", "cls")),
            P(None, ("dom", "cls")),
            P(),
        ),
        out_specs=(P(None, ("dom", "cls"), None), P("cls", None)),
        check_vma=False,
    )
```

```python
import math

import jax
import jax.numpy as jnp
from jax import lax
from jax.experimental import pallas as pl
from jax.experimental.pallas import tpu as pltpu
from jax.sharding import PartitionSpec as P

RADII = 128
ANGLES = 128
ROT = 64
STEPS = 4
ASTEP = 2


def _scores_kernel(pt_ref, sel_ref, r_ref, o_ref, split_ref):
    classes = r_ref.shape[1]
    radii = r_ref.shape[2]
    per_dev = o_ref.shape[2]
    lanes = o_ref.shape[3]
    parts = pt_ref.shape[0]
    pt = jnp.concatenate([pt_ref[e] for e in range(parts)], axis=1)
    rows = pt.shape[0] // per_dev
    r_all = r_ref[0].reshape(classes * radii, r_ref.shape[3])
    split_ref[...] = jnp.dot(r_all, sel_ref[...], preferred_element_type=jnp.float32).astype(split_ref.dtype)

    def body(j, carry):
        halves = []
        for h in range(2):
            base = pl.multiple_of((2 * j + h) * radii, radii)
            blk = split_ref[pl.ds(base, radii), :]
            halves.append(jnp.concatenate([blk[:, e * lanes:(e + 1) * lanes] for e in range(parts)], axis=0))
        rhs = jnp.concatenate(halves, axis=1)
        g = jnp.dot(pt, rhs, preferred_element_type=jnp.float32)
        for h in range(2):
            gh = pltpu.roll(g[:, h * lanes:(h + 1) * lanes], 0, 1, stride=1, stride_axis=0)
            o_ref[0, 2 * j + h] = jnp.sum(gh.reshape(per_dev, rows, lanes), axis=1)
        return carry

    lax.fori_loop(0, classes // 2, body, 0)

def shift_scores(cube, refs, astep):
    n, radii, angles = cube.shape
    steps, classes = refs.shape[:2]
    turns = angles // astep
    b = jnp.arange(angles, dtype=jnp.int32)[None, None, :]
    e = jnp.arange(astep, dtype=jnp.int32)[:, None, None]
    m = jnp.arange(turns, dtype=jnp.int32)[None, :, None]
    pick = (b == astep * ((turns - m) % turns) + e).astype(cube.dtype)
    pt = jnp.einsum("emb,iab->eima", pick, cube, preferred_element_type=jnp.float32)
    pt = pt.astype(cube.dtype).reshape(astep, n * turns, radii)
    b = jnp.arange(angles, dtype=jnp.int32)[:, None]
    col = jnp.arange(astep * 128, dtype=jnp.int32)[None, :]
    sel = (b == astep * ((col % 128) % turns) + col // 128).astype(cube.dtype)
    flops = 2 * steps * classes * (n * turns * radii * astep * 128 + radii * angles * astep * 128)
    return pl.pallas_call(
        _scores_kernel,
        grid=(steps,),
        in_specs=[
            pl.BlockSpec((astep, n * turns, radii), lambda s: (0, 0, 0)),
            pl.BlockSpec((angles, astep * 128), lambda s: (0, 0)),
            pl.BlockSpec((1, classes, radii, angles), lambda s: (s, 0, 0, 0)),
        ],
        out_specs=pl.BlockSpec((1, classes, n, 128), lambda s: (s, 0, 0, 0)),
        out_shape=jax.ShapeDtypeStruct((steps, classes, n, 128), jnp.float32),
        scratch_shapes=[pltpu.VMEM((classes * radii, astep * 128), cube.dtype)],
        cost_estimate=pl.CostEstimate(flops=flops, transcendentals=0, bytes_accessed=pt.size * 2 + refs.size * 2 + steps * classes * n * 128 * 4),
    )(pt, sel, refs)[..., :turns]


def rotate_each(cube, shifts):
    src = jnp.arange(ANGLES, dtype=jnp.int32)
    dst = (src[None, :, None] + shifts[:, None, None]) % ANGLES
    perm = (dst == src[None, None, :]).astype(cube.dtype)
    out = jnp.einsum("iab,ibc->iac", cube, perm, preferred_element_type=jnp.float32)
    return out.astype(cube.dtype)


def per_device(particles, averages, prior_mass, group_ids, class_ids, rot_ids, weights, owners):
    per_dev = particles.shape[0]
    pixels = particles.shape[1]
    groups = lax.axis_size("cls")
    doms = lax.axis_size("dom")
    chunk = pixels // doms
    per_group = averages.shape[0]
    capacity = per_dev * 3 // 8
    slots = groups * capacity
    me_dom = lax.axis_index("dom")
    me_cls = lax.axis_index("cls")
    cube = particles.reshape(per_dev, RADII, ANGLES)
    scale = 1.0 / math.sqrt(pixels)

    rot_all = []
    placing_all = []
    send_wts = []
    for step in range(STEPS):
        shifts = rot_ids[step] * ASTEP
        rot_all.append(rotate_each(cube, shifts).reshape(per_dev, pixels))
        target = group_ids[step, :, 0]
        onehot_group = (target[:, None] == jnp.arange(groups, dtype=jnp.int32)[None, :]).astype(
            jnp.int32
        )
        rank = jnp.sum((jnp.cumsum(onehot_group, axis=0) - 1) * onehot_group, axis=1)
        slot_of = rank * groups + target
        placing = (slot_of[None, :] == jnp.arange(slots, dtype=jnp.int32)[:, None]).astype(
            jnp.bfloat16
        )
        placing_all.append(placing)
        class_hot = (
            class_ids[step][:, None] == jnp.arange(per_group, dtype=jnp.int32)[None, :]
        ).astype(jnp.bfloat16)
        weighted_hot = class_hot * weights[step][:, None]
        wts = jnp.dot(placing, weighted_hot, preferred_element_type=jnp.float32).astype(
            jnp.bfloat16
        )
        wts = jnp.broadcast_to(wts.reshape(capacity, groups, 1, per_group), (capacity, groups, doms, per_group))
        send_wts.append(wts.reshape(capacity, groups * doms, per_group))
    send_img = jnp.einsum(
        "sqi,sip->sqp", jnp.stack(placing_all), jnp.stack(rot_all), preferred_element_type=jnp.float32
    ).astype(jnp.bfloat16)
    send_img = send_img.reshape(STEPS, capacity, groups * doms, chunk)
    send_wts = jnp.stack(send_wts)
    got_img = lax.all_to_all(send_img, ("cls", "dom"), 2, 2, tiled=True)
    got_wts = lax.all_to_all(send_wts, ("cls", "dom"), 2, 2, tiled=True)
    totals = lax.dot_general(
        got_wts, got_img, (((1, 2), (1, 2)), ((0,), (0,))), preferred_element_type=jnp.float32
    )
    mass = jnp.sum(got_wts.astype(jnp.float32), axis=(1, 2))


    current = lax.dynamic_slice_in_dim(averages, me_dom * chunk, chunk, axis=1)
    ref_chunks = []
    for step in range(STEPS):
        current = (prior_mass[:, None] * current + totals[step]) / (prior_mass + mass[step])[:, None]
        ref_chunks.append(current.astype(jnp.bfloat16))
    ref_chunks = jnp.stack(ref_chunks, axis=0)
    ref_chunks = jnp.broadcast_to(ref_chunks[None], (groups,) + ref_chunks.shape)
    got_refs = lax.all_to_all(ref_chunks, "cls", 0, 0, tiled=True)
    owner_hot = (owners[None, :] == jnp.arange(groups, dtype=jnp.int32)[:, None]).astype(jnp.bfloat16)
    owner_chunk = jnp.einsum("gs,gskp->skp", owner_hot, got_refs, preferred_element_type=jnp.float32)
    owner_chunk = owner_chunk.astype(jnp.bfloat16)
    all_refs = lax.all_gather(owner_chunk, "dom", axis=2, tiled=False)
    all_refs = all_refs.reshape(STEPS, per_group, pixels)
    current = current + 0.0 * all_refs[0, 0, 0].astype(jnp.float32)
    final = lax.all_gather(current, "dom", axis=0, tiled=False)
    final = final.transpose(1, 0, 2).reshape(per_group, pixels)

    shifted = shift_scores(cube, all_refs.reshape(STEPS, per_group, RADII, ANGLES), ASTEP)
    scores = shifted.transpose(0, 2, 3, 1).reshape(STEPS, per_dev, ROT * per_group)
    return (scores * scale, final)


def solution(mesh):
    return jax.shard_map(
        per_device,
        mesh=mesh,
        in_specs=(
            P(("dom", "cls"), None),
            P("cls", None),
            P("cls"),
            P(None, ("dom", "cls"), None),
            P(None, ("dom", "cls")),
            P(None, ("dom", "cls")),
            P(None, ("dom", "cls")),
            P(),
        ),
        out_specs=(P(None, ("dom", "cls"), None), P("cls", None)),
        check_vma=False,
    )
```

```python
import math

import jax
import jax.numpy as jnp
from jax import lax
from jax.experimental import pallas as pl
from jax.experimental.pallas import tpu as pltpu
from jax.sharding import PartitionSpec as P

RADII = 128
ANGLES = 128
ROT = 64
STEPS = 4
ASTEP = 2


def _scores_kernel(pt_ref, sel_ref, r_ref, o_ref, split_ref):
    classes = r_ref.shape[1]
    radii = r_ref.shape[2]
    per_dev = o_ref.shape[2]
    lanes = o_ref.shape[3]
    parts = pt_ref.shape[0]
    pt = jnp.concatenate([pt_ref[e] for e in range(parts)], axis=1)
    rows = pt.shape[0] // per_dev
    r_all = r_ref[0].reshape(classes * radii, r_ref.shape[3])
    split_ref[...] = jnp.dot(r_all, sel_ref[...], preferred_element_type=jnp.float32).astype(split_ref.dtype)

    def body(j, carry):
        halves = []
        for h in range(2):
            base = pl.multiple_of((2 * j + h) * radii, radii)
            blk = split_ref[pl.ds(base, radii), :]
            halves.append(jnp.concatenate([blk[:, e * lanes:(e + 1) * lanes] for e in range(parts)], axis=0))
        rhs = jnp.concatenate(halves, axis=1)
        g = jnp.dot(pt, rhs, preferred_element_type=jnp.float32)
        for h in range(2):
            gh = pltpu.roll(g[:, h * lanes:(h + 1) * lanes], 0, 1, stride=1, stride_axis=0)
            o_ref[0, 2 * j + h] = jnp.sum(gh.reshape(per_dev, rows, lanes), axis=1)
        return carry

    lax.fori_loop(0, classes // 2, body, 0)

def shift_scores(cube, refs, astep):
    n, radii, angles = cube.shape
    steps, classes = refs.shape[:2]
    turns = angles // astep
    b = jnp.arange(angles, dtype=jnp.int32)[None, None, :]
    e = jnp.arange(astep, dtype=jnp.int32)[:, None, None]
    m = jnp.arange(turns, dtype=jnp.int32)[None, :, None]
    pick = (b == astep * ((turns - m) % turns) + e).astype(cube.dtype)
    pt = jnp.einsum("emb,iab->eima", pick, cube, preferred_element_type=jnp.float32)
    pt = pt.astype(cube.dtype).reshape(astep, n * turns, radii)
    b = jnp.arange(angles, dtype=jnp.int32)[:, None]
    col = jnp.arange(astep * 128, dtype=jnp.int32)[None, :]
    sel = (b == astep * ((col % 128) % turns) + col // 128).astype(cube.dtype)
    flops = 2 * steps * classes * (n * turns * radii * astep * 128 + radii * angles * astep * 128)
    return pl.pallas_call(
        _scores_kernel,
        grid=(steps,),
        in_specs=[
            pl.BlockSpec((astep, n * turns, radii), lambda s: (0, 0, 0)),
            pl.BlockSpec((angles, astep * 128), lambda s: (0, 0)),
            pl.BlockSpec((1, classes, radii, angles), lambda s: (s, 0, 0, 0)),
        ],
        out_specs=pl.BlockSpec((1, classes, n, 128), lambda s: (s, 0, 0, 0)),
        out_shape=jax.ShapeDtypeStruct((steps, classes, n, 128), jnp.float32),
        scratch_shapes=[pltpu.VMEM((classes * radii, astep * 128), cube.dtype)],
        cost_estimate=pl.CostEstimate(flops=flops, transcendentals=0, bytes_accessed=pt.size * 2 + refs.size * 2 + steps * classes * n * 128 * 4),
    )(pt, sel, refs)[..., :turns]


def rotate_each(cube, shifts):
    src = jnp.arange(ANGLES, dtype=jnp.int32)
    dst = (src[None, :, None] + shifts[:, None, None]) % ANGLES
    perm = (dst == src[None, None, :]).astype(cube.dtype)
    out = jnp.einsum("iab,ibc->iac", cube, perm, preferred_element_type=jnp.float32)
    return out.astype(cube.dtype)


def per_device(particles, averages, prior_mass, group_ids, class_ids, rot_ids, weights, owners):
    per_dev = particles.shape[0]
    pixels = particles.shape[1]
    groups = lax.axis_size("cls")
    doms = lax.axis_size("dom")
    chunk = pixels // doms
    per_group = averages.shape[0]
    capacity = per_dev * 3 // 8
    slots = groups * capacity
    me_dom = lax.axis_index("dom")
    me_cls = lax.axis_index("cls")
    cube = particles.reshape(per_dev, RADII, ANGLES)
    scale = 1.0 / math.sqrt(pixels)

    send_img = []
    send_wts = []
    for step in range(STEPS):
        shifts = rot_ids[step] * ASTEP
        rotated = rotate_each(cube, shifts).reshape(per_dev, pixels)
        target = group_ids[step, :, 0]
        onehot_group = (target[:, None] == jnp.arange(groups, dtype=jnp.int32)[None, :]).astype(
            jnp.int32
        )
        rank = jnp.sum((jnp.cumsum(onehot_group, axis=0) - 1) * onehot_group, axis=1)
        slot_of = target * capacity + rank
        placing = (slot_of[None, :] == jnp.arange(slots, dtype=jnp.int32)[:, None]).astype(
            jnp.bfloat16
        )
        images = jnp.dot(placing, rotated, preferred_element_type=jnp.float32).astype(jnp.bfloat16)
        images = images.reshape(groups, capacity, doms, chunk).transpose(2, 0, 1, 3)
        send_img.append(images)
        class_hot = (
            class_ids[step][:, None] == jnp.arange(per_group, dtype=jnp.int32)[None, :]
        ).astype(jnp.bfloat16)
        weighted_hot = class_hot * weights[step][:, None]
        wts = jnp.dot(placing, weighted_hot, preferred_element_type=jnp.float32).astype(
            jnp.bfloat16
        )
        wts = jnp.broadcast_to(wts.reshape(1, groups, capacity, per_group), (doms, groups, capacity, per_group))
        send_wts.append(wts)
    send_img = jnp.stack(send_img, axis=2).reshape(doms * groups, STEPS, capacity, chunk)
    send_wts = jnp.stack(send_wts, axis=2).reshape(doms * groups, STEPS, capacity, per_group)
    got_img = lax.all_to_all(send_img, ("dom", "cls"), 0, 0, tiled=True)
    got_wts = lax.all_to_all(send_wts, ("dom", "cls"), 0, 0, tiled=True)
    totals = lax.dot_general(
        got_wts, got_img, (((0, 2), (0, 2)), ((1,), (1,))), preferred_element_type=jnp.float32
    )
    mass = jnp.sum(got_wts.astype(jnp.float32), axis=(0, 2))

    current = lax.dynamic_slice_in_dim(averages, me_dom * chunk, chunk, axis=1)
    ref_chunks = []
    for step in range(STEPS):
        current = (prior_mass[:, None] * current + totals[step]) / (prior_mass + mass[step])[:, None]
        ref_chunks.append(current.astype(jnp.bfloat16))
    ref_chunks = jnp.stack(ref_chunks, axis=0).reshape(STEPS, per_group, chunk // ANGLES, ANGLES)
    ref_chunks = jnp.broadcast_to(ref_chunks[None], (groups,) + ref_chunks.shape)
    got_refs = lax.all_to_all(ref_chunks, "cls", 0, 0, tiled=True)
    owner_hot = (owners[None, :] == jnp.arange(groups, dtype=jnp.int32)[:, None]).astype(jnp.bfloat16)
    owner_chunk = jnp.einsum("gs,gskrc->skrc", owner_hot, got_refs, preferred_element_type=jnp.float32)
    owner_chunk = owner_chunk.astype(jnp.bfloat16)
    gathered = lax.all_gather(owner_chunk, "dom", axis=2, tiled=False)
    current = current + 0.0 * gathered[0, 0, 0, 0, 0].astype(jnp.float32)
    all_refs = gathered.reshape(STEPS, per_group, pixels)
    final = lax.all_gather(current, "dom", axis=1, tiled=False).reshape(per_group, pixels)

    shifted = shift_scores(cube, all_refs.reshape(STEPS, per_group, RADII, ANGLES), ASTEP)
    scores = shifted.transpose(0, 2, 3, 1).reshape(STEPS, per_dev, ROT * per_group)
    return (scores * scale, final)


def solution(mesh):
    return jax.shard_map(
        per_device,
        mesh=mesh,
        in_specs=(
            P(("dom", "cls"), None),
            P("cls", None),
            P("cls"),
            P(None, ("dom", "cls"), None),
            P(None, ("dom", "cls")),
            P(None, ("dom", "cls")),
            P(None, ("dom", "cls")),
            P(),
        ),
        out_specs=(P(None, ("dom", "cls"), None), P("cls", None)),
        check_vma=False,
    )
```

```python
import math

import jax
import jax.numpy as jnp
from jax import lax
from jax.experimental import pallas as pl
from jax.experimental.pallas import tpu as pltpu
from jax.sharding import PartitionSpec as P

RADII = 128
ANGLES = 128
ROT = 64
STEPS = 4
ASTEP = 2


def _scores_kernel(pt_ref, sel_ref, r_ref, o_ref, split_ref):
    classes = r_ref.shape[1]
    radii = r_ref.shape[2]
    per_dev = o_ref.shape[2]
    lanes = o_ref.shape[3]
    parts = pt_ref.shape[0]
    pt = jnp.concatenate([pt_ref[e] for e in range(parts)], axis=1)
    rows = pt.shape[0] // per_dev
    r_all = r_ref[0].reshape(classes * radii, r_ref.shape[3])
    split_ref[...] = jnp.dot(r_all, sel_ref[...], preferred_element_type=jnp.float32).astype(split_ref.dtype)

    def body(j, carry):
        halves = []
        for h in range(2):
            base = pl.multiple_of((2 * j + h) * radii, radii)
            blk = split_ref[pl.ds(base, radii), :]
            halves.append(jnp.concatenate([blk[:, e * lanes:(e + 1) * lanes] for e in range(parts)], axis=0))
        rhs = jnp.concatenate(halves, axis=1)
        g = jnp.dot(pt, rhs, preferred_element_type=jnp.float32)
        for h in range(2):
            gh = pltpu.roll(g[:, h * lanes:(h + 1) * lanes], 0, 1, stride=1, stride_axis=0)
            o_ref[0, 2 * j + h] = jnp.sum(gh.reshape(per_dev, rows, lanes), axis=1)
        return carry

    lax.fori_loop(0, classes // 2, body, 0)

def shift_scores(cube, refs, astep):
    n, radii, angles = cube.shape
    steps, classes = refs.shape[:2]
    turns = angles // astep
    b = jnp.arange(angles, dtype=jnp.int32)[None, None, :]
    e = jnp.arange(astep, dtype=jnp.int32)[:, None, None]
    m = jnp.arange(turns, dtype=jnp.int32)[None, :, None]
    pick = (b == astep * ((turns - m) % turns) + e).astype(cube.dtype)
    pt = jnp.einsum("emb,iab->eima", pick, cube, preferred_element_type=jnp.float32)
    pt = pt.astype(cube.dtype).reshape(astep, n * turns, radii)
    b = jnp.arange(angles, dtype=jnp.int32)[:, None]
    col = jnp.arange(astep * 128, dtype=jnp.int32)[None, :]
    sel = (b == astep * ((col % 128) % turns) + col // 128).astype(cube.dtype)
    flops = 2 * steps * classes * (n * turns * radii * astep * 128 + radii * angles * astep * 128)
    return pl.pallas_call(
        _scores_kernel,
        grid=(steps,),
        in_specs=[
            pl.BlockSpec((astep, n * turns, radii), lambda s: (0, 0, 0)),
            pl.BlockSpec((angles, astep * 128), lambda s: (0, 0)),
            pl.BlockSpec((1, classes, radii, angles), lambda s: (s, 0, 0, 0)),
        ],
        out_specs=pl.BlockSpec((1, classes, n, 128), lambda s: (s, 0, 0, 0)),
        out_shape=jax.ShapeDtypeStruct((steps, classes, n, 128), jnp.float32),
        scratch_shapes=[pltpu.VMEM((classes * radii, astep * 128), cube.dtype)],
        cost_estimate=pl.CostEstimate(flops=flops, transcendentals=0, bytes_accessed=pt.size * 2 + refs.size * 2 + steps * classes * n * 128 * 4),
    )(pt, sel, refs)[..., :turns]


def rotate_each(cube, shifts):
    src = jnp.arange(ANGLES, dtype=jnp.int32)
    dst = (src[None, :, None] + shifts[:, None, None]) % ANGLES
    perm = (dst == src[None, None, :]).astype(cube.dtype)
    out = jnp.einsum("iab,ibc->iac", cube, perm, preferred_element_type=jnp.float32)
    return out.astype(cube.dtype)


def per_device(particles, averages, prior_mass, group_ids, class_ids, rot_ids, weights, owners):
    per_dev = particles.shape[0]
    pixels = particles.shape[1]
    groups = lax.axis_size("cls")
    doms = lax.axis_size("dom")
    chunk = pixels // doms
    per_group = averages.shape[0]
    capacity = per_dev * 3 // 8
    slots = groups * capacity
    me_dom = lax.axis_index("dom")
    me_cls = lax.axis_index("cls")
    cube = particles.reshape(per_dev, RADII, ANGLES)
    scale = 1.0 / math.sqrt(pixels)

    send_img = []
    send_wts = []
    for step in range(STEPS):
        shifts = rot_ids[step] * ASTEP
        rotated = rotate_each(cube, shifts).reshape(per_dev, pixels)
        target = group_ids[step, :, 0]
        onehot_group = (target[:, None] == jnp.arange(groups, dtype=jnp.int32)[None, :]).astype(
            jnp.int32
        )
        rank = jnp.sum((jnp.cumsum(onehot_group, axis=0) - 1) * onehot_group, axis=1)
        slot_of = target * capacity + rank
        placing = (slot_of[None, :] == jnp.arange(slots, dtype=jnp.int32)[:, None]).astype(
            jnp.bfloat16
        )
        images = jnp.dot(placing, rotated, preferred_element_type=jnp.float32).astype(jnp.bfloat16)
        images = images.reshape(groups, capacity, doms, chunk).transpose(2, 0, 1, 3)
        send_img.append(images)
        class_hot = (
            class_ids[step][:, None] == jnp.arange(per_group, dtype=jnp.int32)[None, :]
        ).astype(jnp.bfloat16)
        weighted_hot = class_hot * weights[step][:, None]
        wts = jnp.dot(placing, weighted_hot, preferred_element_type=jnp.float32).astype(
            jnp.bfloat16
        )
        wts = jnp.broadcast_to(wts.reshape(1, groups, capacity, per_group), (doms, groups, capacity, per_group))
        send_wts.append(wts)
    send_img = jnp.stack(send_img, axis=2).reshape(doms * groups, STEPS, capacity, chunk)
    send_wts = jnp.stack(send_wts, axis=2).reshape(doms * groups, STEPS, capacity, per_group)
    dests = doms * groups
    img_len = capacity * chunk
    wts_len = capacity * per_group
    pad = -wts_len % 128
    packed = jnp.concatenate(
        [
            send_img.reshape(dests, STEPS, img_len),
            send_wts.reshape(dests, STEPS, wts_len),
            jnp.zeros((dests, STEPS, pad), jnp.bfloat16),
        ],
        axis=2,
    )
    got = lax.all_to_all(packed, ("dom", "cls"), 0, 0, tiled=True)
    got_img = got[:, :, :img_len].reshape(dests, STEPS, capacity, chunk)
    got_wts = got[:, :, img_len:img_len + wts_len].reshape(dests, STEPS, capacity, per_group)
    totals = lax.dot_general(
        got_wts, got_img, (((0, 2), (0, 2)), ((1,), (1,))), preferred_element_type=jnp.float32
    )
    mass = jnp.sum(got_wts.astype(jnp.float32), axis=(0, 2))

    current = lax.dynamic_slice_in_dim(averages, me_dom * chunk, chunk, axis=1)
    ref_chunks = []
    for step in range(STEPS):
        current = (prior_mass[:, None] * current + totals[step]) / (prior_mass + mass[step])[:, None]
        ref_chunks.append(current.astype(jnp.bfloat16))
    ref_chunks = jnp.stack(ref_chunks, axis=0)
    ref_chunks = jnp.broadcast_to(ref_chunks[None], (groups,) + ref_chunks.shape)
    got_refs = lax.all_to_all(ref_chunks, "cls", 0, 0, tiled=True)
    owner_hot = (owners[None, :] == jnp.arange(groups, dtype=jnp.int32)[:, None]).astype(jnp.bfloat16)
    owner_chunk = jnp.einsum("gs,gskp->skp", owner_hot, got_refs, preferred_element_type=jnp.float32)
    owner_chunk = owner_chunk.astype(jnp.bfloat16)
    all_refs = lax.all_gather(owner_chunk, "dom", axis=2, tiled=False)
    all_refs = all_refs.reshape(STEPS, per_group, pixels)
    current = current + 0.0 * all_refs[0, 0, 0].astype(jnp.float32)
    final = lax.all_gather(current, "dom", axis=0, tiled=False)
    final = final.transpose(1, 0, 2).reshape(per_group, pixels)

    shifted = shift_scores(cube, all_refs.reshape(STEPS, per_group, RADII, ANGLES), ASTEP)
    scores = shifted.transpose(0, 2, 3, 1).reshape(STEPS, per_dev, ROT * per_group)
    return (scores * scale, final)


def solution(mesh):
    return jax.shard_map(
        per_device,
        mesh=mesh,
        in_specs=(
            P(("dom", "cls"), None),
            P("cls", None),
            P("cls"),
            P(None, ("dom", "cls"), None),
            P(None, ("dom", "cls")),
            P(None, ("dom", "cls")),
            P(None, ("dom", "cls")),
            P(),
        ),
        out_specs=(P(None, ("dom", "cls"), None), P("cls", None)),
        check_vma=False,
    )
```

```python
import functools
import math

import jax
import jax.numpy as jnp
from jax import lax
from jax.experimental import pallas as pl
from jax.experimental.pallas import tpu as pltpu
from jax.sharding import PartitionSpec as P

RADII = 128
ANGLES = 128
ROT = 64
STEPS = 4
ASTEP = 2


def _scores_kernel(scale, pt_ref, sel_ref, r_ref, o_ref, split_ref):
    classes = r_ref.shape[1]
    radii = r_ref.shape[2]
    per_dev = o_ref.shape[2]
    lanes = o_ref.shape[3]
    parts = pt_ref.shape[0]
    pt = jnp.concatenate([pt_ref[e] for e in range(parts)], axis=1)
    rows = pt.shape[0] // per_dev
    r_all = r_ref[0].reshape(classes * radii, r_ref.shape[3])
    split_ref[...] = jnp.dot(r_all, sel_ref[...], preferred_element_type=jnp.float32).astype(split_ref.dtype)

    def body(j, carry):
        halves = []
        for h in range(2):
            base = pl.multiple_of((2 * j + h) * radii, radii)
            blk = split_ref[pl.ds(base, radii), :]
            halves.append(jnp.concatenate([blk[:, e * lanes:(e + 1) * lanes] for e in range(parts)], axis=0))
        rhs = jnp.concatenate(halves, axis=1)
        g = jnp.dot(pt, rhs, preferred_element_type=jnp.float32)
        for h in range(2):
            gh = pltpu.roll(g[:, h * lanes:(h + 1) * lanes], 0, 1, stride=1, stride_axis=0)
            o_ref[0, 2 * j + h] = jnp.sum(gh.reshape(per_dev, rows, lanes), axis=1) * scale
        return carry

    lax.fori_loop(0, classes // 2, body, 0)

def shift_scores(cube, refs, astep):
    n, radii, angles = cube.shape
    steps, classes = refs.shape[:2]
    turns = angles // astep
    b = jnp.arange(angles, dtype=jnp.int32)[None, None, :]
    e = jnp.arange(astep, dtype=jnp.int32)[:, None, None]
    m = jnp.arange(turns, dtype=jnp.int32)[None, :, None]
    pick = (b == astep * ((turns - m) % turns) + e).astype(cube.dtype)
    pt = jnp.einsum("emb,iab->eima", pick, cube, preferred_element_type=jnp.float32)
    pt = pt.astype(cube.dtype).reshape(astep, n * turns, radii)
    b = jnp.arange(angles, dtype=jnp.int32)[:, None]
    col = jnp.arange(astep * 128, dtype=jnp.int32)[None, :]
    sel = (b == astep * ((col % 128) % turns) + col // 128).astype(cube.dtype)
    flops = 2 * steps * classes * (n * turns * radii * astep * 128 + radii * angles * astep * 128)
    return pl.pallas_call(
        functools.partial(_scores_kernel, 1.0 / math.sqrt(radii * angles)),
        grid=(steps,),
        in_specs=[
            pl.BlockSpec((astep, n * turns, radii), lambda s: (0, 0, 0)),
            pl.BlockSpec((angles, astep * 128), lambda s: (0, 0)),
            pl.BlockSpec((1, classes, radii, angles), lambda s: (s, 0, 0, 0)),
        ],
        out_specs=pl.BlockSpec((1, classes, n, 128), lambda s: (s, 0, 0, 0)),
        out_shape=jax.ShapeDtypeStruct((steps, classes, n, 128), jnp.float32),
        scratch_shapes=[pltpu.VMEM((classes * radii, astep * 128), cube.dtype)],
        cost_estimate=pl.CostEstimate(flops=flops, transcendentals=0, bytes_accessed=pt.size * 2 + refs.size * 2 + steps * classes * n * 128 * 4),
    )(pt, sel, refs)[..., :turns]


def rotate_each(cube, shifts):
    src = jnp.arange(ANGLES, dtype=jnp.int32)
    dst = (src[None, :, None] + shifts[:, None, None]) % ANGLES
    perm = (dst == src[None, None, :]).astype(cube.dtype)
    out = jnp.einsum("iab,ibc->iac", cube, perm, preferred_element_type=jnp.float32)
    return out.astype(cube.dtype)


def per_device(particles, averages, prior_mass, group_ids, class_ids, rot_ids, weights, owners):
    per_dev = particles.shape[0]
    pixels = particles.shape[1]
    groups = lax.axis_size("cls")
    doms = lax.axis_size("dom")
    chunk = pixels // doms
    per_group = averages.shape[0]
    capacity = per_dev * 3 // 8
    slots = groups * capacity
    me_dom = lax.axis_index("dom")
    me_cls = lax.axis_index("cls")
    cube = particles.reshape(per_dev, RADII, ANGLES)
    scale = 1.0 / math.sqrt(pixels)

    send_img = []
    send_wts = []
    for step in range(STEPS):
        shifts = rot_ids[step] * ASTEP
        rotated = rotate_each(cube, shifts).reshape(per_dev, pixels)
        target = group_ids[step, :, 0]
        onehot_group = (target[:, None] == jnp.arange(groups, dtype=jnp.int32)[None, :]).astype(
            jnp.int32
        )
        rank = jnp.sum((jnp.cumsum(onehot_group, axis=0) - 1) * onehot_group, axis=1)
        slot_of = target * capacity + rank
        placing = (slot_of[None, :] == jnp.arange(slots, dtype=jnp.int32)[:, None]).astype(
            jnp.bfloat16
        )
        images = jnp.dot(placing, rotated, preferred_element_type=jnp.float32).astype(jnp.bfloat16)
        images = images.reshape(groups, capacity, doms, chunk).transpose(2, 0, 1, 3)
        send_img.append(images)
        class_hot = (
            class_ids[step][:, None] == jnp.arange(per_group, dtype=jnp.int32)[None, :]
        ).astype(jnp.bfloat16)
        weighted_hot = class_hot * weights[step][:, None]
        wts = jnp.dot(placing, weighted_hot, preferred_element_type=jnp.float32).astype(
            jnp.bfloat16
        )
        wts = jnp.broadcast_to(wts.reshape(1, groups, capacity, per_group), (doms, groups, capacity, per_group))
        send_wts.append(wts)
    send_img = jnp.stack(send_img, axis=2).reshape(doms * groups, STEPS, capacity, chunk)
    send_wts = jnp.stack(send_wts, axis=2).reshape(doms * groups, STEPS, capacity, per_group)
    got_img = lax.all_to_all(send_img, ("dom", "cls"), 0, 0, tiled=True)
    got_wts = lax.all_to_all(send_wts, ("dom", "cls"), 0, 0, tiled=True)
    totals = lax.dot_general(
        got_wts, got_img, (((0, 2), (0, 2)), ((1,), (1,))), preferred_element_type=jnp.float32
    )
    mass = jnp.sum(got_wts.astype(jnp.float32), axis=(0, 2))

    current = lax.dynamic_slice_in_dim(averages, me_dom * chunk, chunk, axis=1)
    ref_chunks = []
    for step in range(STEPS):
        current = (prior_mass[:, None] * current + totals[step]) / (prior_mass + mass[step])[:, None]
        ref_chunks.append(current.astype(jnp.bfloat16))
    ref_chunks = jnp.stack(ref_chunks, axis=0)
    ref_chunks = jnp.broadcast_to(ref_chunks[None], (groups,) + ref_chunks.shape)
    got_refs = lax.all_to_all(ref_chunks, "cls", 0, 0, tiled=True)
    owner_hot = (owners[None, :] == jnp.arange(groups, dtype=jnp.int32)[:, None]).astype(jnp.bfloat16)
    owner_chunk = jnp.einsum("gs,gskp->skp", owner_hot, got_refs, preferred_element_type=jnp.float32)
    owner_chunk = owner_chunk.astype(jnp.bfloat16)
    all_refs = lax.all_gather(owner_chunk, "dom", axis=2, tiled=False)
    all_refs = all_refs.reshape(STEPS, per_group, pixels)
    current = current + 0.0 * all_refs[0, 0, 0].astype(jnp.float32)
    final = lax.all_gather(current, "dom", axis=0, tiled=False)
    final = final.transpose(1, 0, 2).reshape(per_group, pixels)

    shifted = shift_scores(cube, all_refs.reshape(STEPS, per_group, RADII, ANGLES), ASTEP)
    scores = shifted.transpose(0, 2, 3, 1).reshape(STEPS, per_dev, ROT * per_group)
    return (scores, final)


def solution(mesh):
    return jax.shard_map(
        per_device,
        mesh=mesh,
        in_specs=(
            P(("dom", "cls"), None),
            P("cls", None),
            P("cls"),
            P(None, ("dom", "cls"), None),
            P(None, ("dom", "cls")),
            P(None, ("dom", "cls")),
            P(None, ("dom", "cls")),
            P(),
        ),
        out_specs=(P(None, ("dom", "cls"), None), P("cls", None)),
        check_vma=False,
    )
```

```python
import math

import jax
import jax.numpy as jnp
from jax import lax
from jax.experimental import pallas as pl
from jax.experimental.pallas import tpu as pltpu
from jax.sharding import PartitionSpec as P

RADII = 128
ANGLES = 128
ROT = 64
STEPS = 4
ASTEP = 2


def _scores_kernel(pt_ref, sel_ref, r_ref, o_ref, split_ref):
    classes = r_ref.shape[1]
    radii = r_ref.shape[2]
    per_dev = o_ref.shape[2]
    lanes = o_ref.shape[3]
    parts = pt_ref.shape[0]
    pt = jnp.concatenate([pt_ref[e] for e in range(parts)], axis=1)
    rows = pt.shape[0] // per_dev
    r_all = r_ref[0].reshape(classes * radii, r_ref.shape[3])
    split_ref[...] = jnp.dot(r_all, sel_ref[...], preferred_element_type=jnp.float32).astype(split_ref.dtype)

    def body(j, carry):
        halves = []
        for h in range(2):
            base = pl.multiple_of((2 * j + h) * radii, radii)
            blk = split_ref[pl.ds(base, radii), :]
            halves.append(jnp.concatenate([blk[:, e * lanes:(e + 1) * lanes] for e in range(parts)], axis=0))
        rhs = jnp.concatenate(halves, axis=1)
        g = jnp.dot(pt, rhs, preferred_element_type=jnp.float32)
        for h in range(2):
            gh = pltpu.roll(g[:, h * lanes:(h + 1) * lanes], 0, 1, stride=1, stride_axis=0)
            o_ref[0, 2 * j + h] = jnp.sum(gh.reshape(per_dev, rows, lanes), axis=1)
        return carry

    lax.fori_loop(0, classes // 2, body, 0, unroll=2)

def shift_scores(cube, refs, astep):
    n, radii, angles = cube.shape
    steps, classes = refs.shape[:2]
    turns = angles // astep
    b = jnp.arange(angles, dtype=jnp.int32)[None, None, :]
    e = jnp.arange(astep, dtype=jnp.int32)[:, None, None]
    m = jnp.arange(turns, dtype=jnp.int32)[None, :, None]
    pick = (b == astep * ((turns - m) % turns) + e).astype(cube.dtype)
    pt = jnp.einsum("emb,iab->eima", pick, cube, preferred_element_type=jnp.float32)
    pt = pt.astype(cube.dtype).reshape(astep, n * turns, radii)
    b = jnp.arange(angles, dtype=jnp.int32)[:, None]
    col = jnp.arange(astep * 128, dtype=jnp.int32)[None, :]
    sel = (b == astep * ((col % 128) % turns) + col // 128).astype(cube.dtype)
    flops = 2 * steps * classes * (n * turns * radii * astep * 128 + radii * angles * astep * 128)
    return pl.pallas_call(
        _scores_kernel,
        grid=(steps,),
        in_specs=[
            pl.BlockSpec((astep, n * turns, radii), lambda s: (0, 0, 0)),
            pl.BlockSpec((angles, astep * 128), lambda s: (0, 0)),
            pl.BlockSpec((1, classes, radii, angles), lambda s: (s, 0, 0, 0)),
        ],
        out_specs=pl.BlockSpec((1, classes, n, 128), lambda s: (s, 0, 0, 0)),
        out_shape=jax.ShapeDtypeStruct((steps, classes, n, 128), jnp.float32),
        scratch_shapes=[pltpu.VMEM((classes * radii, astep * 128), cube.dtype)],
        cost_estimate=pl.CostEstimate(flops=flops, transcendentals=0, bytes_accessed=pt.size * 2 + refs.size * 2 + steps * classes * n * 128 * 4),
    )(pt, sel, refs)[..., :turns]


def rotate_each(cube, shifts):
    src = jnp.arange(ANGLES, dtype=jnp.int32)
    dst = (src[None, :, None] + shifts[:, None, None]) % ANGLES
    perm = (dst == src[None, None, :]).astype(cube.dtype)
    out = jnp.einsum("iab,ibc->iac", cube, perm, preferred_element_type=jnp.float32)
    return out.astype(cube.dtype)


def per_device(particles, averages, prior_mass, group_ids, class_ids, rot_ids, weights, owners):
    per_dev = particles.shape[0]
    pixels = particles.shape[1]
    groups = lax.axis_size("cls")
    doms = lax.axis_size("dom")
    chunk = pixels // doms
    per_group = averages.shape[0]
    capacity = per_dev * 3 // 8
    slots = groups * capacity
    me_dom = lax.axis_index("dom")
    me_cls = lax.axis_index("cls")
    cube = particles.reshape(per_dev, RADII, ANGLES)
    scale = 1.0 / math.sqrt(pixels)

    send_img = []
    send_wts = []
    for step in range(STEPS):
        shifts = rot_ids[step] * ASTEP
        rotated = rotate_each(cube, shifts).reshape(per_dev, pixels)
        target = group_ids[step, :, 0]
        onehot_group = (target[:, None] == jnp.arange(groups, dtype=jnp.int32)[None, :]).astype(
            jnp.int32
        )
        rank = jnp.sum((jnp.cumsum(onehot_group, axis=0) - 1) * onehot_group, axis=1)
        slot_of = target * capacity + rank
        placing = (slot_of[None, :] == jnp.arange(slots, dtype=jnp.int32)[:, None]).astype(
            jnp.bfloat16
        )
        images = jnp.dot(placing, rotated, preferred_element_type=jnp.float32).astype(jnp.bfloat16)
        images = images.reshape(groups, capacity, doms, chunk).transpose(2, 0, 1, 3)
        send_img.append(images)
        class_hot = (
            class_ids[step][:, None] == jnp.arange(per_group, dtype=jnp.int32)[None, :]
        ).astype(jnp.bfloat16)
        weighted_hot = class_hot * weights[step][:, None]
        wts = jnp.dot(placing, weighted_hot, preferred_element_type=jnp.float32).astype(
            jnp.bfloat16
        )
        wts = jnp.broadcast_to(wts.reshape(1, groups, capacity, per_group), (doms, groups, capacity, per_group))
        send_wts.append(wts)
    send_img = jnp.stack(send_img, axis=2).reshape(doms * groups, STEPS, capacity, chunk)
    send_wts = jnp.stack(send_wts, axis=2).reshape(doms * groups, STEPS, capacity, per_group)
    got_img = lax.all_to_all(send_img, ("dom", "cls"), 0, 0, tiled=True)
    got_wts = lax.all_to_all(send_wts, ("dom", "cls"), 0, 0, tiled=True)
    totals = lax.dot_general(
        got_wts, got_img, (((0, 2), (0, 2)), ((1,), (1,))), preferred_element_type=jnp.float32
    )
    mass = jnp.sum(got_wts.astype(jnp.float32), axis=(0, 2))

    current = lax.dynamic_slice_in_dim(averages, me_dom * chunk, chunk, axis=1)
    ref_chunks = []
    for step in range(STEPS):
        current = (prior_mass[:, None] * current + totals[step]) / (prior_mass + mass[step])[:, None]
        ref_chunks.append(current.astype(jnp.bfloat16))
    ref_chunks = jnp.stack(ref_chunks, axis=0)
    ref_chunks = jnp.broadcast_to(ref_chunks[None], (groups,) + ref_chunks.shape)
    got_refs = lax.all_to_all(ref_chunks, "cls", 0, 0, tiled=True)
    owner_hot = (owners[None, :] == jnp.arange(groups, dtype=jnp.int32)[:, None]).astype(jnp.bfloat16)
    owner_chunk = jnp.einsum("gs,gskp->skp", owner_hot, got_refs, preferred_element_type=jnp.float32)
    owner_chunk = owner_chunk.astype(jnp.bfloat16)
    all_refs = lax.all_gather(owner_chunk, "dom", axis=2, tiled=False)
    all_refs = all_refs.reshape(STEPS, per_group, pixels)
    current = current + 0.0 * all_refs[0, 0, 0].astype(jnp.float32)
    final = lax.all_gather(current, "dom", axis=0, tiled=False)
    final = final.transpose(1, 0, 2).reshape(per_group, pixels)

    shifted = shift_scores(cube, all_refs.reshape(STEPS, per_group, RADII, ANGLES), ASTEP)
    scores = shifted.transpose(0, 2, 3, 1).reshape(STEPS, per_dev, ROT * per_group)
    return (scores * scale, final)


def solution(mesh):
    return jax.shard_map(
        per_device,
        mesh=mesh,
        in_specs=(
            P(("dom", "cls"), None),
            P("cls", None),
            P("cls"),
            P(None, ("dom", "cls"), None),
            P(None, ("dom", "cls")),
            P(None, ("dom", "cls")),
            P(None, ("dom", "cls")),
            P(),
        ),
        out_specs=(P(None, ("dom", "cls"), None), P("cls", None)),
        check_vma=False,
    )
```

```python
import math

import jax
import jax.numpy as jnp
from jax import lax
from jax.experimental import pallas as pl
from jax.experimental.pallas import tpu as pltpu
from jax.sharding import PartitionSpec as P

RADII = 128
ANGLES = 128
ROT = 64
STEPS = 4
ASTEP = 2


def _scores_kernel(pt_ref, sel_ref, r_ref, o_ref, split_ref):
    classes = r_ref.shape[1]
    radii = r_ref.shape[2]
    per_dev = o_ref.shape[2]
    lanes = o_ref.shape[3]
    parts = pt_ref.shape[0]
    pt = jnp.concatenate([pt_ref[e] for e in range(parts)], axis=1)
    rows = pt.shape[0] // per_dev
    r_all = r_ref[0].reshape(classes * radii, r_ref.shape[3])
    split_ref[...] = jnp.dot(r_all, sel_ref[...], preferred_element_type=jnp.float32).astype(split_ref.dtype)

    def body(j, carry):
        halves = []
        for h in range(2):
            base = pl.multiple_of((2 * j + h) * radii, radii)
            blk = split_ref[pl.ds(base, radii), :]
            halves.append(jnp.concatenate([blk[:, e * lanes:(e + 1) * lanes] for e in range(parts)], axis=0))
        rhs = jnp.concatenate(halves, axis=1)
        g = jnp.dot(pt, rhs, preferred_element_type=jnp.float32)
        for h in range(2):
            gh = pltpu.roll(g[:, h * lanes:(h + 1) * lanes], 0, 1, stride=1, stride_axis=0)
            o_ref[0, 2 * j + h] = jnp.sum(gh.reshape(per_dev, rows, lanes), axis=1)
        return carry

    lax.fori_loop(0, classes // 2, body, 0, unroll=2)

def shift_scores(cube, refs, astep):
    n, radii, angles = cube.shape
    steps, classes = refs.shape[:2]
    turns = angles // astep
    b = jnp.arange(angles, dtype=jnp.int32)[None, None, :]
    e = jnp.arange(astep, dtype=jnp.int32)[:, None, None]
    m = jnp.arange(turns, dtype=jnp.int32)[None, :, None]
    pick = (b == astep * ((turns - m) % turns) + e).astype(cube.dtype)
    pt = jnp.einsum("emb,iab->eima", pick, cube, preferred_element_type=jnp.float32)
    pt = pt.astype(cube.dtype).reshape(astep, n * turns, radii)
    b = jnp.arange(angles, dtype=jnp.int32)[:, None]
    col = jnp.arange(astep * 128, dtype=jnp.int32)[None, :]
    sel = (b == astep * ((col % 128) % turns) + col // 128).astype(cube.dtype)
    flops = 2 * steps * classes * (n * turns * radii * astep * 128 + radii * angles * astep * 128)
    return pl.pallas_call(
        _scores_kernel,
        grid=(steps,),
        in_specs=[
            pl.BlockSpec((astep, n * turns, radii), lambda s: (0, 0, 0)),
            pl.BlockSpec((angles, astep * 128), lambda s: (0, 0)),
            pl.BlockSpec((1, classes, radii, angles), lambda s: (s, 0, 0, 0)),
        ],
        out_specs=pl.BlockSpec((1, classes, n, 128), lambda s: (s, 0, 0, 0)),
        out_shape=jax.ShapeDtypeStruct((steps, classes, n, 128), jnp.float32),
        scratch_shapes=[pltpu.VMEM((classes * radii, astep * 128), cube.dtype)],
        cost_estimate=pl.CostEstimate(flops=flops, transcendentals=0, bytes_accessed=pt.size * 2 + refs.size * 2 + steps * classes * n * 128 * 4),
    )(pt, sel, refs)[..., :turns]


def rotate_each(cube, shifts):
    src = jnp.arange(ANGLES, dtype=jnp.int32)
    dst = (src[None, :, None] + shifts[:, None, None]) % ANGLES
    perm = (dst == src[None, None, :]).astype(cube.dtype)
    out = jnp.einsum("iab,ibc->iac", cube, perm, preferred_element_type=jnp.float32)
    return out.astype(cube.dtype)


def per_device(particles, averages, prior_mass, group_ids, class_ids, rot_ids, weights, owners):
    per_dev = particles.shape[0]
    pixels = particles.shape[1]
    groups = lax.axis_size("cls")
    doms = lax.axis_size("dom")
    chunk = pixels // doms
    per_group = averages.shape[0]
    capacity = per_dev * 3 // 8
    slots = groups * capacity
    me_dom = lax.axis_index("dom")
    me_cls = lax.axis_index("cls")
    cube = particles.reshape(per_dev, RADII, ANGLES)
    scale = 1.0 / math.sqrt(pixels)

    send_img = []
    send_wts = []
    for step in range(STEPS):
        shifts = rot_ids[step] * ASTEP
        rotated = rotate_each(cube, shifts).reshape(per_dev, pixels)
        target = group_ids[step, :, 0]
        onehot_group = (target[:, None] == jnp.arange(groups, dtype=jnp.int32)[None, :]).astype(
            jnp.int32
        )
        rank = jnp.sum((jnp.cumsum(onehot_group, axis=0) - 1) * onehot_group, axis=1)
        slot_of = target * capacity + rank
        placing = (slot_of[None, :] == jnp.arange(slots, dtype=jnp.int32)[:, None]).astype(
            jnp.bfloat16
        )
        images = jnp.dot(placing, rotated, preferred_element_type=jnp.float32).astype(jnp.bfloat16)
        images = images.reshape(groups, capacity, doms, chunk).transpose(2, 0, 1, 3)
        send_img.append(images)
        class_hot = (
            class_ids[step][:, None] == jnp.arange(per_group, dtype=jnp.int32)[None, :]
        ).astype(jnp.bfloat16)
        weighted_hot = class_hot * weights[step][:, None]
        wts = jnp.dot(placing, weighted_hot, preferred_element_type=jnp.float32).astype(
            jnp.bfloat16
        )
        wts = jnp.broadcast_to(wts.reshape(1, groups, capacity, per_group), (doms, groups, capacity, per_group))
        send_wts.append(wts)
    send_img = jnp.stack(send_img, axis=2).reshape(doms * groups, STEPS, capacity, chunk)
    send_wts = jnp.stack(send_wts, axis=2).reshape(doms * groups, STEPS, capacity, per_group)
    got_img = lax.all_to_all(send_img, ("dom", "cls"), 0, 0, tiled=True)
    got_wts = lax.all_to_all(send_wts, ("dom", "cls"), 0, 0, tiled=True)
    totals = lax.dot_general(
        got_wts, got_img, (((0, 2), (0, 2)), ((1,), (1,))), preferred_element_type=jnp.float32
    )
    mass = jnp.sum(got_wts.astype(jnp.float32), axis=(0, 2))

    current = lax.dynamic_slice_in_dim(averages, me_dom * chunk, chunk, axis=1)
    ref_chunks = []
    for step in range(STEPS):
        current = (prior_mass[:, None] * current + totals[step]) / (prior_mass + mass[step])[:, None]
        ref_chunks.append(current.astype(jnp.bfloat16))
    ref_chunks = jnp.stack(ref_chunks, axis=0)
    ref_chunks = jnp.broadcast_to(ref_chunks[None], (groups,) + ref_chunks.shape)
    got_refs = lax.all_to_all(ref_chunks, "cls", 0, 0, tiled=True)
    owner_hot = (owners[None, :] == jnp.arange(groups, dtype=jnp.int32)[:, None]).astype(jnp.bfloat16)
    owner_chunk = jnp.einsum("gs,gskp->skp", owner_hot, got_refs, preferred_element_type=jnp.float32)
    owner_chunk = owner_chunk.astype(jnp.bfloat16)
    all_refs = lax.all_gather(owner_chunk, "dom", axis=2, tiled=False)
    all_refs = all_refs.reshape(STEPS, per_group, pixels)
    final = lax.all_to_all(jnp.broadcast_to(current[None], (doms,) + current.shape), "dom", 0, 0, tiled=True)
    final = final.transpose(1, 0, 2).reshape(per_group, pixels)

    shifted = shift_scores(cube, all_refs.reshape(STEPS, per_group, RADII, ANGLES), ASTEP)
    scores = shifted.transpose(0, 2, 3, 1).reshape(STEPS, per_dev, ROT * per_group)
    return (scores * scale, final)


def solution(mesh):
    return jax.shard_map(
        per_device,
        mesh=mesh,
        in_specs=(
            P(("dom", "cls"), None),
            P("cls", None),
            P("cls"),
            P(None, ("dom", "cls"), None),
            P(None, ("dom", "cls")),
            P(None, ("dom", "cls")),
            P(None, ("dom", "cls")),
            P(),
        ),
        out_specs=(P(None, ("dom", "cls"), None), P("cls", None)),
        check_vma=False,
    )
```
